32 devices in a mesh: row: 4 (over x, core), col: 8 (over z, y).
Axes of the slice: x: 2, y: 2, z: 4, core: 2. Of those that a mesh axis runs over, the one named last changes fastest.
Arguments:
- right_side: float32 [64, 16384], P(None, 'row'), may hold values from -8 to 8
- blocks: bfloat16 [3072, 128, 128], P(('row', 'col')), may hold values from -1 to 1
- targets: int32 [3072, 1], P(('row', 'col')), may hold values from 0 to 7; in each aligned block of 96 rows (0 to 95, 96 to 191, ...) at most 24 rows name the same one
- tile_rows: int32 [3072], P(('row', 'col')), may hold values from 0 to 31
- tile_cols: int32 [3072], P(('row', 'col')), may hold values from 0 to 31
Outputs:
- solution: float32 [64, 8, 4096], P(None, 'col', 'row')
- phibar: float32 [64], replicated
The draws below stay inside these ranges and needn't reach their ends.
Inputs may be any that keep to these rules, and one draw needn't show every extreme that they name: `targets`: among the 96 blocks of one device, at most 24 name the same grid column, and some grid column is named exactly 24 times by some device.
All inputs are finite; a program needn't handle non-finite values.
Results may differ from the reference program's by a relative error of at most 0.0032.
Values may be sent and summed in bfloat16 or wider, within the bound.
No kernel may reach another device: no remote copies, remote signals or barrier semaphores. Data moves between devices by JAX's collectives and lax.ppermute only.
A program may use at most 128 MiB of HBM per device.

```python
import math
import jax
import jax.numpy as jnp
import numpy as np
from jax import lax

BLK = 128
SNAP = 64
TR = 32
TC = 32
NB_SRC = 96
ITERS = 4
CAP = 24
CT = 4096
M = 16384
N = 32768
NBLK = 3072
N_ROW = 4
N_COL = 8


level_span = 1.5


level_norm = 1.8274


entry_clip = 4.0


def level_logs(key, salt):
    return jax.random.uniform(jax.random.fold_in(key, salt), (BLK,), jnp.float32, -level_span, level_span)


def bounded_entries(key, shape):
    return jnp.clip(jax.random.normal(key, shape, jnp.float32), -entry_clip, entry_clip)


def draw_blocks(key, part):
    row_level = jnp.exp(level_logs(key, 101)) / level_norm
    col_level = jnp.exp(level_logs(key, 102)) / level_norm
    fan_count = BLK * BLK * NBLK / M
    entries = bounded_entries(jax.random.fold_in(key, 103), (NBLK, BLK, BLK))
    scaled = entries * fan_count ** (-0.5) * row_level[None, :, None] * col_level[None, None, :]
    return scaled.astype(jnp.bfloat16)


def draw_right_side(key, part):
    row_logs = level_logs(key, 101)
    exponents = jax.random.uniform(jax.random.fold_in(key, 105), (SNAP,), jnp.float32, -1.0, 1.0)
    weights = jnp.exp(exponents[:, None] * row_logs[None, :])
    tiled = jnp.tile(weights, (1, M // BLK))
    entries = bounded_entries(jax.random.fold_in(key, 104), (SNAP, M))
    return jnp.clip(entries * tiled, -8.0, 8.0).astype(jnp.float32)


def with_ends(drawn, own_key, least, largest):
    longest = drawn.shape.index(max(drawn.shape))
    spots = []
    for shift in (0, 1):
        where = [jax.random.randint(jax.random.fold_in(own_key, axis), (), 0, length) for axis, length in enumerate(drawn.shape)]
        where[longest] = (where[longest] + shift) % drawn.shape[longest]
        spots.append(tuple(where))
    return drawn.at[spots[0]].set(least).at[spots[1]].set(largest)


def deal_out(rng, own, number, rows, count, top, limit, slope):
    sequence = jax.random.permutation(rng, count)
    heavy_load, ordinary = shares(count, rows * top, limit, slope, True), shares(count, rows * top, limit, slope, False)
    places = jnp.arange(count)

    def named(tallies, rotation):
        used = int((tallies > 0).sum())
        fixed = max(1, used // 4)
        shifted = fixed + (places - fixed + rotation * (used - fixed)) % max(1, count - fixed)
        return jnp.zeros((count,), jnp.int32).at[sequence[jnp.where(places < fixed, places, shifted)]].set(jnp.asarray(tallies, jnp.int32))

    tallies = jnp.where(number % 4 == 0, named(heavy_load, number // 4), named(ordinary, number - number // 4 - 1))
    mixed = jax.random.permutation(jax.random.fold_in(own, 3), count)
    source_of, sink = mixed[0:count // 2 * 2:2], mixed[1:count // 2 * 2:2]
    slack = jnp.minimum(tallies[source_of] - 1, limit - tallies[sink]) // 2
    slack = jnp.where((source_of == sequence[0]) | (sink == sequence[0]) | (tallies[sink] == 0), 0, jnp.maximum(slack, 0))
    shifted = jax.random.randint(jax.random.fold_in(own, 4), (count // 2,), 0, 1 << 20) % (slack + 1)
    tallies = tallies.at[source_of].add(-shifted).at[sink].add(shifted)
    labels = jnp.searchsorted(jnp.cumsum(tallies), jnp.arange(rows * top), side="right").astype(jnp.int32)
    table = labels.reshape(top, rows).T
    table = table[jax.random.permutation(jax.random.fold_in(own, 1), rows)]
    rotation = jax.random.randint(jax.random.fold_in(own, 2), (rows, 1), 0, top)
    return jnp.take_along_axis(table, (jnp.arange(top)[None, :] + rotation) % top, axis=1)


def shares(count, total, limit, slope, full):
    weights = [(1 << 20) // math.isqrt(grade ** slope) + 1 for grade in range(1, count + 1)]
    largest = limit if full else min(limit, max(-(-total // count), total * weights[0] // sum(weights)))
    least = 1 if total - largest >= count - 1 else 0
    given, rest = [largest] + [least] * (count - 1), total - largest - least * (count - 1)
    while rest > 0:
        candidates = [i for i in range(1, count) if given[i] < largest] or [i for i in range(1, count) if given[i] < limit]
        mass, remaining = sum([weights[i] for i in candidates]), rest
        for i in candidates:
            addition = min(limit - given[i], max(1, remaining * weights[i] // mass), rest)
            given[i] = given[i] + addition
            rest = rest - addition
    return np.array(given)


def setup_inputs(seed: int = 0) -> dict:
    keys = jax.random.split(jax.random.key(seed), 6)
    right_side = draw_right_side(jax.random.fold_in(keys[5], 71), 0)
    blocks = draw_blocks(jax.random.fold_in(keys[5], 71), 0)
    targets_keys = jax.random.split(jax.random.fold_in(keys[2], 1), NBLK // NB_SRC)
    targets_turns = jax.random.permutation(jax.random.fold_in(keys[2], 3), NBLK // NB_SRC)
    targets = jax.vmap(lambda own, number: deal_out(jax.random.fold_in(keys[2], 2), own, number, NB_SRC, N_COL, 1, CAP, 2))(targets_keys, targets_turns).reshape((NBLK, 1))
    tile_rows = with_ends(jax.random.randint(keys[3], (NBLK,), 0, TR), jax.random.fold_in(keys[3], 1), 0, TR - 1).astype(jnp.int32)
    tile_cols = with_ends(jax.random.randint(keys[4], (NBLK,), 0, TC), jax.random.fold_in(keys[4], 1), 0, TC - 1).astype(jnp.int32)
    return {"right_side": right_side, "blocks": blocks, "targets": targets, "tile_rows": tile_rows, "tile_cols": tile_cols}


EPSILON = 1e-06

def reference(right_side, blocks, targets, tile_rows, tile_cols):
    groups = N_ROW * N_COL
    position = jnp.arange(NBLK, dtype=jnp.int32)
    grid_row = position // (NB_SRC * N_COL)
    row_tile = (grid_row * TR + tile_rows).astype(jnp.int32).reshape(groups, NB_SRC)
    col_tile = (targets[:, 0] * TC + tile_cols).astype(jnp.int32).reshape(groups, NB_SRC)
    grouped = blocks.reshape(groups, NB_SRC, BLK, BLK)

    def forward(right_bf):
        vector_tiles = right_bf.astype(jnp.float32).reshape(SNAP, N // BLK, BLK)

        def apply_group(totals, member):
            tile_block, rows_here, cols_here = member
            picked = jnp.take(vector_tiles, cols_here, axis=1)
            weighted = jnp.einsum('sij,ksj->ksi', tile_block.astype(jnp.float32), picked, precision=lax.Precision.HIGHEST)
            return (totals.at[:, rows_here].add(weighted), None)
        start = jnp.zeros((SNAP, M // BLK, BLK), jnp.float32)
        totals, unused = lax.scan(apply_group, start, (grouped, row_tile, col_tile))
        return totals.reshape(SNAP, M)

    def backward(left_bf):
        vector_tiles = left_bf.astype(jnp.float32).reshape(SNAP, M // BLK, BLK)

        def apply_group(totals, member):
            tile_block, rows_here, cols_here = member
            picked = jnp.take(vector_tiles, rows_here, axis=1)
            weighted = jnp.einsum('sji,ksj->ksi', tile_block.astype(jnp.float32), picked, precision=lax.Precision.HIGHEST)
            return (totals.at[:, cols_here].add(weighted), None)
        start = jnp.zeros((SNAP, N // BLK, BLK), jnp.float32)
        totals, unused = lax.scan(apply_group, start, (grouped, row_tile, col_tile))
        return totals.reshape(SNAP, N)

    def vector_norm(family):
        return jnp.sqrt(lax.optimization_barrier(jnp.sum(family * family, axis=1)) + EPSILON)
    beta_norm = vector_norm(right_side)
    left_vec = right_side / beta_norm[:, None]
    unscaled = backward(left_vec.astype(jnp.bfloat16))
    alpha_norm = vector_norm(unscaled)
    right_vec = unscaled / alpha_norm[:, None]
    search = right_vec
    solution = jnp.zeros((SNAP, N), jnp.float32)
    phibar = beta_norm
    rhobar = alpha_norm
    for iteration in range(ITERS):
        unscaled = forward(right_vec.astype(jnp.bfloat16)) - alpha_norm[:, None] * left_vec
        beta_norm = vector_norm(unscaled)
        left_vec = unscaled / beta_norm[:, None]
        rho_value = jnp.sqrt(rhobar * rhobar + beta_norm * beta_norm)
        cosine = rhobar / rho_value
        sine_value = beta_norm / rho_value
        phi_value = cosine * phibar
        phibar = sine_value * phibar
        solution = solution + (phi_value / rho_value)[:, None] * search
        if iteration + 1 < ITERS:
            unscaled = backward(left_vec.astype(jnp.bfloat16)) - beta_norm[:, None] * right_vec
            alpha_norm = vector_norm(unscaled)
            right_vec = unscaled / alpha_norm[:, None]
            theta_value = sine_value * alpha_norm
            rhobar = -cosine * alpha_norm
            search = right_vec - (theta_value / rho_value)[:, None] * search
    return (solution.reshape(SNAP, N_COL, CT), phibar)
```

```python
import jax
import jax.numpy as jnp
from jax import lax
from jax.sharding import PartitionSpec as P

TC = 32
ITERS = 4


EPSILON = 1e-06


def partner_pairs(count, distance):
    return [(i, i ^ distance) for i in range(count)]


def is_power_of_two(count):
    return count & (count - 1) == 0


def small_sum(value, axis):
    count = lax.axis_size(axis)
    if not is_power_of_two(count):
        return lax.psum(value, axis)
    distance = 1
    while distance < count:
        value = value + lax.ppermute(value, axis, partner_pairs(count, distance))
        distance *= 2
    return value


def big_sum(value, axis):
    count = lax.axis_size(axis)
    width = value.shape[-1]
    if not is_power_of_two(count) or width % (128 * count):
        return lax.psum(value, axis)
    index = lax.axis_index(axis)
    distances = []
    distance = 1
    while distance < count:
        distances.append(distance)
        distance *= 2
    held = value
    for distance in distances:
        half = held.shape[-1] // 2
        upper = (index // distance) % 2
        keep = lax.dynamic_slice_in_dim(held, upper * half, half, held.ndim - 1)
        give = lax.dynamic_slice_in_dim(held, (1 - upper) * half, half, held.ndim - 1)
        held = keep + lax.ppermute(give, axis, partner_pairs(count, distance))
    for distance in reversed(distances):
        upper = (index // distance) % 2
        other = lax.ppermute(held, axis, partner_pairs(count, distance))
        held = jnp.where(
            upper == 1,
            jnp.concatenate([other, held], axis=-1),
            jnp.concatenate([held, other], axis=-1),
        )
    return held


def gather_tiles(vector_bf, indices, block_size):
    snapshots, extent = vector_bf.shape
    vector_tiles = vector_bf.reshape(snapshots, extent // block_size, block_size)
    return jnp.take(vector_tiles, indices, axis=1)


def place_terms(weighted, indices, n_out):
    snapshots, number, block_size = weighted.shape
    onehot = (indices[:, None] == jnp.arange(n_out, dtype=jnp.int32)[None, :]).astype(jnp.float32)
    summed = jnp.einsum("ksi,st->kti", weighted, onehot, precision=lax.Precision.HIGHEST)
    return summed.reshape(snapshots, n_out * block_size)


def forward_terms(vector_bf, blocks, row_index, col_index, n_out):
    picked = gather_tiles(vector_bf, col_index, blocks.shape[1])
    weighted = jnp.einsum("sij,ksj->ksi", blocks, picked, preferred_element_type=jnp.float32)
    return place_terms(weighted, row_index, n_out)


def backward_terms(vector_bf, blocks, row_index, col_index, n_out):
    picked = gather_tiles(vector_bf, row_index, blocks.shape[1])
    weighted = jnp.einsum("sji,ksj->ksi", blocks, picked, preferred_element_type=jnp.float32)
    return place_terms(weighted, col_index, n_out)


def per_device(right_side, blocks, targets, tile_rows, tile_cols):
    col_count = lax.axis_size("col")
    row_count = lax.axis_size("row")
    block_size = blocks.shape[1]
    snapshots = right_side.shape[0]
    row_tiles = right_side.shape[1] // block_size
    own_count = blocks.shape[0]
    capacity = 2 * own_count // col_count
    target = targets[:, 0]
    matches = (target[:, None] == jnp.arange(col_count, dtype=jnp.int32)[None, :]).astype(jnp.int32)
    before = jnp.cumsum(matches, axis=0) - matches
    slot_index = target * capacity + jnp.sum(before * matches, axis=1)
    outgoing = (
        jnp.zeros((col_count * capacity, block_size, block_size), blocks.dtype)
        .at[slot_index]
        .set(blocks)
    )
    places = (
        jnp.zeros((col_count * capacity, 2), jnp.int32)
        .at[slot_index]
        .set(jnp.stack([tile_rows, tile_cols], axis=1))
    )
    arrived, arrived_places = (
        lax.all_to_all(
            outgoing.reshape(col_count, capacity, block_size, block_size),
            "col",
            split_axis=0,
            concat_axis=0,
            tiled=True,
        ),
        lax.all_to_all(
            places.reshape(col_count, capacity, 2), "col", split_axis=0, concat_axis=0, tiled=True
        ),
    )
    work_blocks = arrived.reshape(col_count * capacity, block_size, block_size)
    flat_places = arrived_places.reshape(col_count * capacity, 2)
    work_rows = flat_places[:, 0]
    work_cols = flat_places[:, 1]

    def backward(left_bf):
        return backward_terms(left_bf, work_blocks, work_rows, work_cols, TC)

    def sum_right(partial_value):
        return big_sum(partial_value, "row")

    def finish_left(unscaled, need_form):
        squares = jnp.sum(unscaled * unscaled, axis=1)
        total = small_sum(squares, "row")
        beta_norm = jnp.sqrt(total + EPSILON)
        scaled = unscaled / beta_norm[:, None]
        rounded = None
        if need_form:
            rounded = scaled.astype(jnp.bfloat16)
        return (beta_norm, scaled, rounded)

    def finish_right(unscaled):
        squares = jnp.sum(unscaled * unscaled, axis=1)
        total = small_sum(squares, "col")
        alpha_norm = jnp.sqrt(total + EPSILON)
        scaled = unscaled / alpha_norm[:, None]
        rounded = scaled.astype(jnp.bfloat16)
        return (alpha_norm, scaled, rounded)

    beta_norm, left_vec, left_bf = finish_left(right_side, True)
    alpha_norm, right_vec, right_bf = finish_right(sum_right(backward(left_bf)))
    search = right_vec
    solution = jnp.zeros_like(right_vec)
    phibar = beta_norm
    rhobar = alpha_norm
    for iteration in range(ITERS):
        last_turn = iteration + 1 == ITERS
        unscaled = (
            big_sum(forward_terms(right_bf, work_blocks, work_rows, work_cols, row_tiles), "col")
            - alpha_norm[:, None] * left_vec
        )
        beta_norm, left_vec, left_bf = finish_left(unscaled, not last_turn)
        rho_value = jnp.sqrt(rhobar * rhobar + beta_norm * beta_norm)
        cosine = rhobar / rho_value
        sine_value = beta_norm / rho_value
        phi_value = cosine * phibar
        phibar = sine_value * phibar
        solution = solution + (phi_value / rho_value)[:, None] * search
        if not last_turn:
            unscaled = sum_right(backward(left_bf)) - beta_norm[:, None] * right_vec
            alpha_norm, right_vec, right_bf = finish_right(unscaled)
            theta_value = sine_value * alpha_norm
            rhobar = -cosine * alpha_norm
            search = right_vec - (theta_value / rho_value)[:, None] * search
    share_len = solution.shape[1] // row_count
    solution = lax.dynamic_slice_in_dim(solution, lax.axis_index("row") * share_len, share_len, 1)
    return (solution.reshape(snapshots, 1, solution.shape[1]), phibar)


def solution(mesh):
    placed = (
        P(None, "row"),
        P(("row", "col"), None, None),
        P(("row", "col"), None),
        P(("row", "col")),
        P(("row", "col")),
    )
    return jax.shard_map(
        per_device,
        mesh=mesh,
        in_specs=placed,
        out_specs=(P(None, "col", "row"), P()),
        check_vma=False,
    )
```

```python
import jax
import jax.numpy as jnp
from jax import lax
from jax.sharding import PartitionSpec as P

TC = 32
ITERS = 4
CHUNKS = 2


EPSILON = 1e-06


def partner_pairs(count, distance):
    return [(i, i ^ distance) for i in range(count)]


def is_power_of_two(count):
    return count & (count - 1) == 0


def small_sum(value, axis):
    count = lax.axis_size(axis)
    if not is_power_of_two(count):
        return lax.psum(value, axis)
    distance = 1
    while distance < count:
        value = value + lax.ppermute(value, axis, partner_pairs(count, distance))
        distance *= 2
    return value


def big_sum(value, axis):
    count = lax.axis_size(axis)
    width = value.shape[-1]
    if not is_power_of_two(count) or width % (128 * count):
        return lax.psum(value, axis)
    index = lax.axis_index(axis)
    distances = []
    distance = 1
    while distance < count:
        distances.append(distance)
        distance *= 2
    held = value
    for distance in distances:
        half = held.shape[-1] // 2
        upper = (index // distance) % 2
        keep = lax.dynamic_slice_in_dim(held, upper * half, half, held.ndim - 1)
        give = lax.dynamic_slice_in_dim(held, (1 - upper) * half, half, held.ndim - 1)
        held = keep + lax.ppermute(give, axis, partner_pairs(count, distance))
    for distance in reversed(distances):
        upper = (index // distance) % 2
        other = lax.ppermute(held, axis, partner_pairs(count, distance))
        held = jnp.where(
            upper == 1,
            jnp.concatenate([other, held], axis=-1),
            jnp.concatenate([held, other], axis=-1),
        )
    return held


def gather_tiles(vector_bf, indices, block_size):
    snapshots, extent = vector_bf.shape
    vector_tiles = vector_bf.reshape(snapshots, extent // block_size, block_size)
    return jnp.take(vector_tiles, indices, axis=1)


def place_terms(weighted, indices, n_out):
    snapshots, number, block_size = weighted.shape
    onehot = (indices[:, None] == jnp.arange(n_out, dtype=jnp.int32)[None, :]).astype(jnp.float32)
    summed = jnp.einsum("ksi,st->kti", weighted, onehot, precision=lax.Precision.HIGHEST)
    return summed.reshape(snapshots, n_out * block_size)


def forward_terms(vector_bf, blocks, row_index, col_index, n_out):
    picked = gather_tiles(vector_bf, col_index, blocks.shape[1])
    weighted = jnp.einsum("sij,ksj->ksi", blocks, picked, preferred_element_type=jnp.float32)
    return place_terms(weighted, row_index, n_out)


def backward_terms(vector_bf, blocks, row_index, col_index, n_out):
    picked = gather_tiles(vector_bf, row_index, blocks.shape[1])
    weighted = jnp.einsum("sji,ksj->ksi", blocks, picked, preferred_element_type=jnp.float32)
    return place_terms(weighted, col_index, n_out)


def per_device(right_side, blocks, targets, tile_rows, tile_cols):
    col_count = lax.axis_size("col")
    row_count = lax.axis_size("row")
    block_size = blocks.shape[1]
    snapshots = right_side.shape[0]
    row_tiles = right_side.shape[1] // block_size
    own_count = blocks.shape[0]
    capacity = 2 * own_count // col_count
    target = targets[:, 0]
    matches = (target[:, None] == jnp.arange(col_count, dtype=jnp.int32)[None, :]).astype(jnp.int32)
    before = jnp.cumsum(matches, axis=0) - matches
    slot_index = target * capacity + jnp.sum(before * matches, axis=1)
    outgoing = (
        jnp.zeros((col_count * capacity, block_size, block_size), blocks.dtype)
        .at[slot_index]
        .set(blocks)
    )
    places = (
        jnp.zeros((col_count * capacity, 2), jnp.int32)
        .at[slot_index]
        .set(jnp.stack([tile_rows, tile_cols], axis=1))
    )
    arrived, arrived_places = (
        lax.all_to_all(
            outgoing.reshape(col_count, capacity, block_size, block_size),
            "col",
            split_axis=0,
            concat_axis=0,
            tiled=True,
        ),
        lax.all_to_all(
            places.reshape(col_count, capacity, 2), "col", split_axis=0, concat_axis=0, tiled=True
        ),
    )
    work_blocks = arrived.reshape(col_count * capacity, block_size, block_size)
    flat_places = arrived_places.reshape(col_count * capacity, 2)
    work_rows = flat_places[:, 0]
    work_cols = flat_places[:, 1]

    def backward(left_bf):
        return backward_terms(left_bf, work_blocks, work_rows, work_cols, TC)

    def sum_right(partial_value):
        return big_sum(partial_value, "row")

    def finish_left(unscaled, need_form):
        squares = jnp.sum(unscaled * unscaled, axis=1)
        total = small_sum(squares, "row")
        beta_norm = jnp.sqrt(total + EPSILON)
        scaled = unscaled / beta_norm[:, None]
        rounded = None
        if need_form:
            rounded = scaled.astype(jnp.bfloat16)
        return (beta_norm, scaled, rounded)

    def finish_right(unscaled):
        squares = jnp.sum(unscaled * unscaled, axis=1)
        total = small_sum(squares, "col")
        alpha_norm = jnp.sqrt(total + EPSILON)
        scaled = unscaled / alpha_norm[:, None]
        rounded = scaled.astype(jnp.bfloat16)
        return (alpha_norm, scaled, rounded)

    def run_chunk(side, results):
        beta_norm, left_vec, left_bf = finish_left(side, True)
        yield
        alpha_norm, right_vec, right_bf = finish_right(sum_right(backward(left_bf)))
        yield
        search = right_vec
        solution = jnp.zeros_like(right_vec)
        phibar = beta_norm
        rhobar = alpha_norm
        for iteration in range(ITERS):
            last_turn = iteration + 1 == ITERS
            unscaled = (
                big_sum(forward_terms(right_bf, work_blocks, work_rows, work_cols, row_tiles), "col")
                - alpha_norm[:, None] * left_vec
            )
            beta_norm, left_vec, left_bf = finish_left(unscaled, not last_turn)
            rho_value = jnp.sqrt(rhobar * rhobar + beta_norm * beta_norm)
            cosine = rhobar / rho_value
            sine_value = beta_norm / rho_value
            phi_value = cosine * phibar
            phibar = sine_value * phibar
            solution = solution + (phi_value / rho_value)[:, None] * search
            yield
            if not last_turn:
                unscaled = sum_right(backward(left_bf)) - beta_norm[:, None] * right_vec
                alpha_norm, right_vec, right_bf = finish_right(unscaled)
                theta_value = sine_value * alpha_norm
                rhobar = -cosine * alpha_norm
                search = right_vec - (theta_value / rho_value)[:, None] * search
                yield
        results.append((solution, phibar))

    chunk_len = snapshots // CHUNKS
    results = [[] for _ in range(CHUNKS)]
    runs = [
        run_chunk(right_side[k * chunk_len:(k + 1) * chunk_len], results[k])
        for k in range(CHUNKS)
    ]
    active = list(runs)
    while active:
        still = []
        for run in active:
            try:
                next(run)
                still.append(run)
            except StopIteration:
                pass
        active = still
    solution = jnp.concatenate([r[0][0] for r in results], axis=0)
    phibar = jnp.concatenate([r[0][1] for r in results], axis=0)
    share_len = solution.shape[1] // row_count
    solution = lax.dynamic_slice_in_dim(solution, lax.axis_index("row") * share_len, share_len, 1)
    return (solution.reshape(snapshots, 1, solution.shape[1]), phibar)


def solution(mesh):
    placed = (
        P(None, "row"),
        P(("row", "col"), None, None),
        P(("row", "col"), None),
        P(("row", "col")),
        P(("row", "col")),
    )
    return jax.shard_map(
        per_device,
        mesh=mesh,
        in_specs=placed,
        out_specs=(P(None, "col", "row"), P()),
        check_vma=False,
    )
```

```python
import jax
import jax.numpy as jnp
from jax import lax
from jax.sharding import PartitionSpec as P

TC = 32
ITERS = 4
CHUNKS = 2


EPSILON = 1e-06


def partner_pairs(count, distance):
    return [(i, i ^ distance) for i in range(count)]


def is_power_of_two(count):
    return count & (count - 1) == 0


def small_sum(value, axis):
    count = lax.axis_size(axis)
    if not is_power_of_two(count):
        return lax.psum(value, axis)
    distance = 1
    while distance < count:
        value = value + lax.ppermute(value, axis, partner_pairs(count, distance))
        distance *= 2
    return value


def big_sum(value, axis):
    count = lax.axis_size(axis)
    width = value.shape[-1]
    if not is_power_of_two(count) or width % (128 * count):
        return lax.psum(value, axis)
    index = lax.axis_index(axis)
    distances = []
    distance = 1
    while distance < count:
        distances.append(distance)
        distance *= 2
    held = value
    for distance in distances:
        half = held.shape[-1] // 2
        upper = (index // distance) % 2
        keep = lax.dynamic_slice_in_dim(held, upper * half, half, held.ndim - 1)
        give = lax.dynamic_slice_in_dim(held, (1 - upper) * half, half, held.ndim - 1)
        held = keep + lax.ppermute(give, axis, partner_pairs(count, distance))
    for distance in reversed(distances):
        upper = (index // distance) % 2
        other = lax.ppermute(held, axis, partner_pairs(count, distance))
        held = jnp.where(
            upper == 1,
            jnp.concatenate([other, held], axis=-1),
            jnp.concatenate([held, other], axis=-1),
        )
    return held


def gather_tiles(vector_bf, indices, block_size):
    snapshots, extent = vector_bf.shape
    vector_tiles = vector_bf.reshape(snapshots, extent // block_size, block_size)
    return jnp.take(vector_tiles, indices, axis=1)


def place_terms(weighted, indices, n_out):
    snapshots, number, block_size = weighted.shape
    onehot = (indices[:, None] == jnp.arange(n_out, dtype=jnp.int32)[None, :]).astype(jnp.float32)
    summed = jnp.einsum("ksi,st->kti", weighted, onehot, precision=lax.Precision.HIGHEST)
    return summed.reshape(snapshots, n_out * block_size)


def forward_terms(vector_bf, blocks, row_index, col_index, n_out):
    picked = gather_tiles(vector_bf, col_index, blocks.shape[1])
    weighted = jnp.einsum("sij,ksj->ksi", blocks, picked, preferred_element_type=jnp.float32)
    return place_terms(weighted, row_index, n_out)


def backward_terms(vector_bf, blocks, row_index, col_index, n_out):
    picked = gather_tiles(vector_bf, row_index, blocks.shape[1])
    weighted = jnp.einsum("sji,ksj->ksi", blocks, picked, preferred_element_type=jnp.float32)
    return place_terms(weighted, col_index, n_out)


def per_device(right_side, blocks, targets, tile_rows, tile_cols):
    col_count = lax.axis_size("col")
    row_count = lax.axis_size("row")
    block_size = blocks.shape[1]
    snapshots = right_side.shape[0]
    row_tiles = right_side.shape[1] // block_size
    own_count = blocks.shape[0]
    capacity = 2 * own_count // col_count
    target = targets[:, 0]
    matches = (target[:, None] == jnp.arange(col_count, dtype=jnp.int32)[None, :]).astype(jnp.int32)
    before = jnp.cumsum(matches, axis=0) - matches
    slot_index = target * capacity + jnp.sum(before * matches, axis=1)
    outgoing = (
        jnp.zeros((col_count * capacity, block_size, block_size), blocks.dtype)
        .at[slot_index]
        .set(blocks)
    )
    places = (
        jnp.zeros((col_count * capacity, 2), jnp.int32)
        .at[slot_index]
        .set(jnp.stack([tile_rows, tile_cols], axis=1))
    )
    arrived, arrived_places = (
        lax.all_to_all(
            outgoing.reshape(col_count, capacity, block_size, block_size),
            "col",
            split_axis=0,
            concat_axis=0,
            tiled=True,
        ),
        lax.all_to_all(
            places.reshape(col_count, capacity, 2), "col", split_axis=0, concat_axis=0, tiled=True
        ),
    )
    work_blocks = arrived.reshape(col_count * capacity, block_size, block_size)
    flat_places = arrived_places.reshape(col_count * capacity, 2)
    work_rows = flat_places[:, 0]
    work_cols = flat_places[:, 1]

    def backward(left_bf):
        return backward_terms(left_bf, work_blocks, work_rows, work_cols, TC)

    def forward(right_bf):
        return forward_terms(right_bf, work_blocks, work_rows, work_cols, row_tiles)

    def sum_left(partial_value):
        return big_sum(partial_value, "col")

    def sum_right(partial_value):
        return big_sum(partial_value, "row")

    def finish_left(unscaled, need_form):
        squares = jnp.sum(unscaled * unscaled, axis=1)
        total = small_sum(squares, "row")
        beta_norm = jnp.sqrt(total + EPSILON)
        scaled = unscaled / beta_norm[:, None]
        rounded = None
        if need_form:
            rounded = scaled.astype(jnp.bfloat16)
        return (beta_norm, scaled, rounded)

    def finish_right(unscaled):
        squares = jnp.sum(unscaled * unscaled, axis=1)
        total = small_sum(squares, "col")
        alpha_norm = jnp.sqrt(total + EPSILON)
        scaled = unscaled / alpha_norm[:, None]
        rounded = scaled.astype(jnp.bfloat16)
        return (alpha_norm, scaled, rounded)

    latest = [None] * CHUNKS

    def staggered(product, summed, vector, chunk):
        if chunk > 0 and latest[chunk - 1] is not None:
            vector, unused = lax.optimization_barrier((vector, latest[chunk - 1]))
        result = summed(product(vector))
        latest[chunk] = result
        return result

    def run_chunk(chunk, side, results):
        beta_norm, left_vec, left_bf = finish_left(side, True)
        yield
        alpha_norm, right_vec, right_bf = finish_right(staggered(backward, sum_right, left_bf, chunk))
        yield
        search = right_vec
        solution = jnp.zeros_like(right_vec)
        phibar = beta_norm
        rhobar = alpha_norm
        for iteration in range(ITERS):
            last_turn = iteration + 1 == ITERS
            unscaled = (
                staggered(forward, sum_left, right_bf, chunk)
                - alpha_norm[:, None] * left_vec
            )
            beta_norm, left_vec, left_bf = finish_left(unscaled, not last_turn)
            rho_value = jnp.sqrt(rhobar * rhobar + beta_norm * beta_norm)
            cosine = rhobar / rho_value
            sine_value = beta_norm / rho_value
            phi_value = cosine * phibar
            phibar = sine_value * phibar
            solution = solution + (phi_value / rho_value)[:, None] * search
            yield
            if not last_turn:
                unscaled = staggered(backward, sum_right, left_bf, chunk) - beta_norm[:, None] * right_vec
                alpha_norm, right_vec, right_bf = finish_right(unscaled)
                theta_value = sine_value * alpha_norm
                rhobar = -cosine * alpha_norm
                search = right_vec - (theta_value / rho_value)[:, None] * search
                yield
        results.append((solution, phibar))

    chunk_len = snapshots // CHUNKS
    results = [[] for _ in range(CHUNKS)]
    runs = [
        run_chunk(k, right_side[k * chunk_len:(k + 1) * chunk_len], results[k])
        for k in range(CHUNKS)
    ]
    active = list(runs)
    while active:
        still = []
        for run in active:
            try:
                next(run)
                still.append(run)
            except StopIteration:
                pass
        active = still
    solution = jnp.concatenate([r[0][0] for r in results], axis=0)
    phibar = jnp.concatenate([r[0][1] for r in results], axis=0)
    share_len = solution.shape[1] // row_count
    solution = lax.dynamic_slice_in_dim(solution, lax.axis_index("row") * share_len, share_len, 1)
    return (solution.reshape(snapshots, 1, solution.shape[1]), phibar)


def solution(mesh):
    placed = (
        P(None, "row"),
        P(("row", "col"), None, None),
        P(("row", "col"), None),
        P(("row", "col")),
        P(("row", "col")),
    )
    return jax.shard_map(
        per_device,
        mesh=mesh,
        in_specs=placed,
        out_specs=(P(None, "col", "row"), P()),
        check_vma=False,
    )
```

```python
import jax
import jax.numpy as jnp
from jax import lax
from jax.sharding import PartitionSpec as P

TC = 32
ITERS = 4
CHUNKS = 2


EPSILON = 1e-06


def partner_pairs(count, distance):
    return [(i, i ^ distance) for i in range(count)]


def is_power_of_two(count):
    return count & (count - 1) == 0


def small_sum(value, axis):
    count = lax.axis_size(axis)
    if not is_power_of_two(count):
        return lax.psum(value, axis)
    distance = 1
    while distance < count:
        value = value + lax.ppermute(value, axis, partner_pairs(count, distance))
        distance *= 2
    return value


def big_sum(value, axis):
    count = lax.axis_size(axis)
    width = value.shape[-1]
    if not is_power_of_two(count) or width % (128 * count):
        return lax.psum(value, axis)
    index = lax.axis_index(axis)
    distances = []
    distance = 1
    while distance < count:
        distances.append(distance)
        distance *= 2
    held = value
    for distance in distances:
        half = held.shape[-1] // 2
        upper = (index // distance) % 2
        keep = lax.dynamic_slice_in_dim(held, upper * half, half, held.ndim - 1)
        give = lax.dynamic_slice_in_dim(held, (1 - upper) * half, half, held.ndim - 1)
        held = keep + lax.ppermute(give, axis, partner_pairs(count, distance))
    for distance in reversed(distances):
        upper = (index // distance) % 2
        other = lax.ppermute(held, axis, partner_pairs(count, distance))
        held = jnp.where(
            upper == 1,
            jnp.concatenate([other, held], axis=-1),
            jnp.concatenate([held, other], axis=-1),
        )
    return held


def gather_tiles(vector_bf, indices, block_size):
    snapshots, extent = vector_bf.shape
    vector_tiles = vector_bf.reshape(snapshots, extent // block_size, block_size)
    return jnp.take(vector_tiles, indices, axis=1)


def place_terms(weighted, indices, n_out):
    snapshots, number, block_size = weighted.shape
    onehot = (indices[:, None] == jnp.arange(n_out, dtype=jnp.int32)[None, :]).astype(jnp.float32)
    summed = jnp.einsum("ksi,st->kti", weighted, onehot, precision=lax.Precision.HIGHEST)
    return summed.reshape(snapshots, n_out * block_size)


def forward_terms(vector_bf, blocks, row_index, col_index, n_out):
    picked = gather_tiles(vector_bf, col_index, blocks.shape[1])
    weighted = jnp.einsum("sij,ksj->ksi", blocks, picked, preferred_element_type=jnp.float32)
    return place_terms(weighted, row_index, n_out)


def backward_terms(vector_bf, blocks, row_index, col_index, n_out):
    picked = gather_tiles(vector_bf, row_index, blocks.shape[1])
    weighted = jnp.einsum("sji,ksj->ksi", blocks, picked, preferred_element_type=jnp.float32)
    return place_terms(weighted, col_index, n_out)


def per_device(right_side, blocks, targets, tile_rows, tile_cols):
    col_count = lax.axis_size("col")
    row_count = lax.axis_size("row")
    block_size = blocks.shape[1]
    snapshots = right_side.shape[0]
    row_tiles = right_side.shape[1] // block_size
    own_count = blocks.shape[0]
    capacity = 2 * own_count // col_count
    target = targets[:, 0]
    slot_count = col_count * capacity

    def slot_of(named):
        matches = (named[..., :, None] == jnp.arange(col_count, dtype=jnp.int32)).astype(jnp.int32)
        before = jnp.cumsum(matches, axis=-2) - matches
        return named * capacity + jnp.sum(before * matches, axis=-1)

    pick = slot_of(target)[:, None] == jnp.arange(slot_count, dtype=jnp.int32)[None, :]
    source = jnp.sum(jnp.where(pick, jnp.arange(own_count, dtype=jnp.int32)[:, None], 0), axis=0)
    filled = jnp.any(pick, axis=0)
    outgoing = jnp.where(filled[:, None, None], jnp.take(blocks, source, axis=0), jnp.zeros((), blocks.dtype))
    arrived = lax.all_to_all(
        outgoing.reshape(col_count, capacity, block_size, block_size),
        "col",
        split_axis=0,
        concat_axis=0,
        tiled=True,
    )
    everyone = lax.all_gather(jnp.stack([target, tile_rows, tile_cols], axis=1), "col")
    wanted = lax.axis_index("col") * capacity + jnp.arange(capacity, dtype=jnp.int32)
    hit = slot_of(everyone[:, :, 0])[:, :, None] == wanted[None, None, :]
    work_rows = jnp.sum(jnp.where(hit, everyone[:, :, 1:2], 0), axis=1).reshape(slot_count)
    work_cols = jnp.sum(jnp.where(hit, everyone[:, :, 2:3], 0), axis=1).reshape(slot_count)
    work_blocks = arrived.reshape(slot_count, block_size, block_size)

    def backward(left_bf):
        return backward_terms(left_bf, work_blocks, work_rows, work_cols, TC)

    def sum_right(partial_value):
        return big_sum(partial_value, "row")

    def finish_left(unscaled, need_form):
        squares = jnp.sum(unscaled * unscaled, axis=1)
        total = small_sum(squares, "row")
        beta_norm = jnp.sqrt(total + EPSILON)
        scaled = unscaled / beta_norm[:, None]
        rounded = None
        if need_form:
            rounded = scaled.astype(jnp.bfloat16)
        return (beta_norm, scaled, rounded)

    def finish_right(unscaled):
        squares = jnp.sum(unscaled * unscaled, axis=1)
        total = small_sum(squares, "col")
        alpha_norm = jnp.sqrt(total + EPSILON)
        scaled = unscaled / alpha_norm[:, None]
        rounded = scaled.astype(jnp.bfloat16)
        return (alpha_norm, scaled, rounded)

    def run_chunk(side, results):
        beta_norm, left_vec, left_bf = finish_left(side, True)
        yield
        alpha_norm, right_vec, right_bf = finish_right(sum_right(backward(left_bf)))
        yield
        search = right_vec
        solution = jnp.zeros_like(right_vec)
        phibar = beta_norm
        rhobar = alpha_norm
        for iteration in range(ITERS):
            last_turn = iteration + 1 == ITERS
            unscaled = (
                big_sum(forward_terms(right_bf, work_blocks, work_rows, work_cols, row_tiles), "col")
                - alpha_norm[:, None] * left_vec
            )
            beta_norm, left_vec, left_bf = finish_left(unscaled, not last_turn)
            rho_value = jnp.sqrt(rhobar * rhobar + beta_norm * beta_norm)
            cosine = rhobar / rho_value
            sine_value = beta_norm / rho_value
            phi_value = cosine * phibar
            phibar = sine_value * phibar
            solution = solution + (phi_value / rho_value)[:, None] * search
            yield
            if not last_turn:
                unscaled = sum_right(backward(left_bf)) - beta_norm[:, None] * right_vec
                alpha_norm, right_vec, right_bf = finish_right(unscaled)
                theta_value = sine_value * alpha_norm
                rhobar = -cosine * alpha_norm
                search = right_vec - (theta_value / rho_value)[:, None] * search
                yield
        results.append((solution, phibar))

    chunk_len = snapshots // CHUNKS
    results = [[] for _ in range(CHUNKS)]
    runs = [
        run_chunk(right_side[k * chunk_len:(k + 1) * chunk_len], results[k])
        for k in range(CHUNKS)
    ]
    active = list(runs)
    while active:
        still = []
        for run in active:
            try:
                next(run)
                still.append(run)
            except StopIteration:
                pass
        active = still
    solution = jnp.concatenate([r[0][0] for r in results], axis=0)
    phibar = jnp.concatenate([r[0][1] for r in results], axis=0)
    share_len = solution.shape[1] // row_count
    solution = lax.dynamic_slice_in_dim(solution, lax.axis_index("row") * share_len, share_len, 1)
    return (solution.reshape(snapshots, 1, solution.shape[1]), phibar)


def solution(mesh):
    placed = (
        P(None, "row"),
        P(("row", "col"), None, None),
        P(("row", "col"), None),
        P(("row", "col")),
        P(("row", "col")),
    )
    return jax.shard_map(
        per_device,
        mesh=mesh,
        in_specs=placed,
        out_specs=(P(None, "col", "row"), P()),
        check_vma=False,
    )
```

```python
import jax
import jax.numpy as jnp
from jax import lax
from jax.sharding import PartitionSpec as P

TC = 32
ITERS = 4
CHUNKS = 2
UNUSED = 1 << 20


EPSILON = 1e-06


def partner_pairs(count, distance):
    return [(i, i ^ distance) for i in range(count)]


def is_power_of_two(count):
    return count & (count - 1) == 0


def small_sum(value, axis):
    count = lax.axis_size(axis)
    if not is_power_of_two(count):
        return lax.psum(value, axis)
    distance = 1
    while distance < count:
        value = value + lax.ppermute(value, axis, partner_pairs(count, distance))
        distance *= 2
    return value


def big_sum(value, axis):
    count = lax.axis_size(axis)
    width = value.shape[-1]
    if not is_power_of_two(count) or width % (128 * count):
        return lax.psum(value, axis)
    index = lax.axis_index(axis)
    distances = []
    distance = 1
    while distance < count:
        distances.append(distance)
        distance *= 2
    held = value
    for distance in distances:
        half = held.shape[-1] // 2
        upper = (index // distance) % 2
        keep = lax.dynamic_slice_in_dim(held, upper * half, half, held.ndim - 1)
        give = lax.dynamic_slice_in_dim(held, (1 - upper) * half, half, held.ndim - 1)
        held = keep + lax.ppermute(give, axis, partner_pairs(count, distance))
    for distance in reversed(distances):
        upper = (index // distance) % 2
        other = lax.ppermute(held, axis, partner_pairs(count, distance))
        held = jnp.where(
            upper == 1,
            jnp.concatenate([other, held], axis=-1),
            jnp.concatenate([held, other], axis=-1),
        )
    return held


def gather_tiles(vector_bf, indices, block_size):
    snapshots, extent = vector_bf.shape
    vector_tiles = vector_bf.reshape(snapshots, extent // block_size, block_size)
    return jnp.take(vector_tiles, indices, axis=1, mode="clip")


def place_terms(weighted, indices, n_out):
    snapshots, number, block_size = weighted.shape
    onehot = (indices[:, None] == jnp.arange(n_out, dtype=jnp.int32)[None, :]).astype(jnp.float32)
    summed = jnp.einsum("ksi,st->kti", weighted, onehot, precision=lax.Precision.HIGHEST)
    return summed.reshape(snapshots, n_out * block_size)


def forward_terms(vector_bf, blocks, row_index, col_index, n_out):
    picked = gather_tiles(vector_bf, col_index, blocks.shape[1])
    weighted = jnp.einsum("sij,ksj->ksi", blocks, picked, preferred_element_type=jnp.float32)
    return place_terms(weighted, row_index, n_out)


def backward_terms(vector_bf, blocks, row_index, col_index, n_out):
    picked = gather_tiles(vector_bf, row_index, blocks.shape[1])
    weighted = jnp.einsum("sji,ksj->ksi", blocks, picked, preferred_element_type=jnp.float32)
    return place_terms(weighted, col_index, n_out)


def per_device(right_side, blocks, targets, tile_rows, tile_cols):
    col_count = lax.axis_size("col")
    row_count = lax.axis_size("row")
    block_size = blocks.shape[1]
    snapshots = right_side.shape[0]
    row_tiles = right_side.shape[1] // block_size
    own_count = blocks.shape[0]
    capacity = 2 * own_count // col_count
    target = targets[:, 0]
    slot_count = col_count * capacity

    def slot_of(named):
        matches = (named[..., :, None] == jnp.arange(col_count, dtype=jnp.int32)).astype(jnp.int32)
        before = jnp.cumsum(matches, axis=-2) - matches
        return named * capacity + jnp.sum(before * matches, axis=-1)

    pick = slot_of(target)[:, None] == jnp.arange(slot_count, dtype=jnp.int32)[None, :]
    source = jnp.sum(jnp.where(pick, jnp.arange(own_count, dtype=jnp.int32)[:, None], 0), axis=0)
    filled = jnp.any(pick, axis=0)
    outgoing = jnp.take(blocks, source, axis=0, mode="clip")
    places = jnp.where(
        filled[:, None],
        jnp.take(jnp.stack([tile_rows, tile_cols], axis=1), source, axis=0, mode="clip"),
        UNUSED,
    )
    arrived = lax.all_to_all(
        outgoing.reshape(col_count, capacity, block_size, block_size),
        "col",
        split_axis=0,
        concat_axis=0,
        tiled=True,
    )
    arrived_places = lax.all_to_all(
        places.reshape(col_count, capacity, 2), "col", split_axis=0, concat_axis=0, tiled=True
    )
    flat_places = arrived_places.reshape(slot_count, 2)
    work_rows = flat_places[:, 0]
    work_cols = flat_places[:, 1]
    work_blocks = arrived.reshape(slot_count, block_size, block_size)

    def backward(left_bf):
        return backward_terms(left_bf, work_blocks, work_rows, work_cols, TC)

    def sum_right(partial_value):
        return big_sum(partial_value, "row")

    def finish_left(unscaled, need_form):
        squares = jnp.sum(unscaled * unscaled, axis=1)
        total = small_sum(squares, "row")
        beta_norm = jnp.sqrt(total + EPSILON)
        scaled = unscaled / beta_norm[:, None]
        rounded = None
        if need_form:
            rounded = scaled.astype(jnp.bfloat16)
        return (beta_norm, scaled, rounded)

    def finish_right(unscaled):
        squares = jnp.sum(unscaled * unscaled, axis=1)
        total = small_sum(squares, "col")
        alpha_norm = jnp.sqrt(total + EPSILON)
        scaled = unscaled / alpha_norm[:, None]
        rounded = scaled.astype(jnp.bfloat16)
        return (alpha_norm, scaled, rounded)

    def run_chunk(side, results):
        beta_norm, left_vec, left_bf = finish_left(side, True)
        yield
        alpha_norm, right_vec, right_bf = finish_right(sum_right(backward(left_bf)))
        yield
        search = right_vec
        solution = jnp.zeros_like(right_vec)
        phibar = beta_norm
        rhobar = alpha_norm
        for iteration in range(ITERS):
            last_turn = iteration + 1 == ITERS
            unscaled = (
                big_sum(forward_terms(right_bf, work_blocks, work_rows, work_cols, row_tiles), "col")
                - alpha_norm[:, None] * left_vec
            )
            beta_norm, left_vec, left_bf = finish_left(unscaled, not last_turn)
            rho_value = jnp.sqrt(rhobar * rhobar + beta_norm * beta_norm)
            cosine = rhobar / rho_value
            sine_value = beta_norm / rho_value
            phi_value = cosine * phibar
            phibar = sine_value * phibar
            solution = solution + (phi_value / rho_value)[:, None] * search
            yield
            if not last_turn:
                unscaled = sum_right(backward(left_bf)) - beta_norm[:, None] * right_vec
                alpha_norm, right_vec, right_bf = finish_right(unscaled)
                theta_value = sine_value * alpha_norm
                rhobar = -cosine * alpha_norm
                search = right_vec - (theta_value / rho_value)[:, None] * search
                yield
        results.append((solution, phibar))

    chunk_len = snapshots // CHUNKS
    results = [[] for _ in range(CHUNKS)]
    runs = [
        run_chunk(right_side[k * chunk_len:(k + 1) * chunk_len], results[k])
        for k in range(CHUNKS)
    ]
    active = list(runs)
    while active:
        still = []
        for run in active:
            try:
                next(run)
                still.append(run)
            except StopIteration:
                pass
        active = still
    solution = jnp.concatenate([r[0][0] for r in results], axis=0)
    phibar = jnp.concatenate([r[0][1] for r in results], axis=0)
    share_len = solution.shape[1] // row_count
    solution = lax.dynamic_slice_in_dim(solution, lax.axis_index("row") * share_len, share_len, 1)
    return (solution.reshape(snapshots, 1, solution.shape[1]), phibar)


def solution(mesh):
    placed = (
        P(None, "row"),
        P(("row", "col"), None, None),
        P(("row", "col"), None),
        P(("row", "col")),
        P(("row", "col")),
    )
    return jax.shard_map(
        per_device,
        mesh=mesh,
        in_specs=placed,
        out_specs=(P(None, "col", "row"), P()),
        check_vma=False,
    )
```

```python
import jax
import jax.numpy as jnp
from jax import lax
from jax.sharding import PartitionSpec as P

TC = 32
ITERS = 4
CHUNKS = 2
UNUSED = 1 << 20


EPSILON = 1e-06


def partner_pairs(count, distance):
    return [(i, i ^ distance) for i in range(count)]


def is_power_of_two(count):
    return count & (count - 1) == 0


def small_sum(value, axis):
    count = lax.axis_size(axis)
    if not is_power_of_two(count):
        return lax.psum(value, axis)
    distance = 1
    while distance < count:
        value = value + lax.ppermute(value, axis, partner_pairs(count, distance))
        distance *= 2
    return value


def big_sum(value, axis):
    count = lax.axis_size(axis)
    width = value.shape[-1]
    if not is_power_of_two(count) or width % (128 * count):
        return lax.psum(value, axis)
    index = lax.axis_index(axis)
    distances = []
    distance = 1
    while distance < count:
        distances.append(distance)
        distance *= 2
    held = value
    for distance in distances:
        half = held.shape[-1] // 2
        upper = (index // distance) % 2
        keep = lax.dynamic_slice_in_dim(held, upper * half, half, held.ndim - 1)
        give = lax.dynamic_slice_in_dim(held, (1 - upper) * half, half, held.ndim - 1)
        held = keep + lax.ppermute(give, axis, partner_pairs(count, distance))
    for distance in reversed(distances):
        upper = (index // distance) % 2
        other = lax.ppermute(held, axis, partner_pairs(count, distance))
        held = jnp.where(
            upper == 1,
            jnp.concatenate([other, held], axis=-1),
            jnp.concatenate([held, other], axis=-1),
        )
    return held


def gather_tiles(vector_bf, indices, block_size):
    snapshots, extent = vector_bf.shape
    vector_tiles = vector_bf.reshape(snapshots, extent // block_size, block_size)
    return jnp.take(vector_tiles, indices, axis=1)


def place_terms(weighted, indices, n_out):
    snapshots, number, block_size = weighted.shape
    onehot = (indices[:, None] == jnp.arange(n_out, dtype=jnp.int32)[None, :]).astype(jnp.float32)
    summed = jnp.einsum("ksi,st->kti", weighted, onehot, precision=lax.Precision.HIGHEST)
    return summed.reshape(snapshots, n_out * block_size)


def forward_terms(vector_bf, blocks, row_index, col_index, n_out):
    picked = gather_tiles(vector_bf, jnp.minimum(col_index, vector_bf.shape[1] // blocks.shape[1] - 1), blocks.shape[1])
    weighted = jnp.einsum("sij,ksj->ksi", blocks, picked, preferred_element_type=jnp.float32)
    return place_terms(weighted, row_index, n_out)


def backward_terms(vector_bf, blocks, row_index, col_index, n_out):
    picked = gather_tiles(vector_bf, jnp.minimum(row_index, vector_bf.shape[1] // blocks.shape[1] - 1), blocks.shape[1])
    weighted = jnp.einsum("sji,ksj->ksi", blocks, picked, preferred_element_type=jnp.float32)
    return place_terms(weighted, col_index, n_out)


def per_device(right_side, blocks, targets, tile_rows, tile_cols):
    col_count = lax.axis_size("col")
    row_count = lax.axis_size("row")
    block_size = blocks.shape[1]
    snapshots = right_side.shape[0]
    row_tiles = right_side.shape[1] // block_size
    own_count = blocks.shape[0]
    capacity = 2 * own_count // col_count
    target = targets[:, 0]
    slot_count = col_count * capacity

    def slot_of(named):
        matches = (named[..., :, None] == jnp.arange(col_count, dtype=jnp.int32)).astype(jnp.int32)
        before = jnp.cumsum(matches, axis=-2) - matches
        return named * capacity + jnp.sum(before * matches, axis=-1)

    pick = slot_of(target)[:, None] == jnp.arange(slot_count, dtype=jnp.int32)[None, :]
    source = jnp.sum(jnp.where(pick, jnp.arange(own_count, dtype=jnp.int32)[:, None], 0), axis=0)
    filled = jnp.any(pick, axis=0)
    outgoing = jnp.take(blocks, source, axis=0, mode="clip")
    places = jnp.where(
        filled[:, None],
        jnp.take(jnp.stack([tile_rows, tile_cols], axis=1), source, axis=0, mode="clip"),
        UNUSED,
    )
    arrived = lax.all_to_all(
        outgoing.reshape(col_count, capacity, block_size, block_size),
        "col",
        split_axis=0,
        concat_axis=0,
        tiled=True,
    )
    arrived_places = lax.all_to_all(
        places.reshape(col_count, capacity, 2), "col", split_axis=0, concat_axis=0, tiled=True
    )
    flat_places = arrived_places.reshape(slot_count, 2)
    work_rows = flat_places[:, 0]
    work_cols = flat_places[:, 1]
    work_blocks = arrived.reshape(slot_count, block_size, block_size)

    def backward(left_bf):
        return backward_terms(left_bf, work_blocks, work_rows, work_cols, TC)

    def sum_right(partial_value):
        return big_sum(partial_value, "row")

    def finish_left(unscaled, need_form):
        squares = jnp.sum(unscaled * unscaled, axis=1)
        total = small_sum(squares, "row")
        beta_norm = jnp.sqrt(total + EPSILON)
        scaled = unscaled / beta_norm[:, None]
        rounded = None
        if need_form:
            rounded = scaled.astype(jnp.bfloat16)
        return (beta_norm, scaled, rounded)

    def finish_right(unscaled):
        squares = jnp.sum(unscaled * unscaled, axis=1)
        total = small_sum(squares, "col")
        alpha_norm = jnp.sqrt(total + EPSILON)
        scaled = unscaled / alpha_norm[:, None]
        rounded = scaled.astype(jnp.bfloat16)
        return (alpha_norm, scaled, rounded)

    def run_chunk(side, results):
        beta_norm, left_vec, left_bf = finish_left(side, True)
        yield
        alpha_norm, right_vec, right_bf = finish_right(sum_right(backward(left_bf)))
        yield
        search = right_vec
        solution = jnp.zeros_like(right_vec)
        phibar = beta_norm
        rhobar = alpha_norm
        for iteration in range(ITERS):
            last_turn = iteration + 1 == ITERS
            unscaled = (
                big_sum(forward_terms(right_bf, work_blocks, work_rows, work_cols, row_tiles), "col")
                - alpha_norm[:, None] * left_vec
            )
            beta_norm, left_vec, left_bf = finish_left(unscaled, not last_turn)
            rho_value = jnp.sqrt(rhobar * rhobar + beta_norm * beta_norm)
            cosine = rhobar / rho_value
            sine_value = beta_norm / rho_value
            phi_value = cosine * phibar
            phibar = sine_value * phibar
            solution = solution + (phi_value / rho_value)[:, None] * search
            yield
            if not last_turn:
                unscaled = sum_right(backward(left_bf)) - beta_norm[:, None] * right_vec
                alpha_norm, right_vec, right_bf = finish_right(unscaled)
                theta_value = sine_value * alpha_norm
                rhobar = -cosine * alpha_norm
                search = right_vec - (theta_value / rho_value)[:, None] * search
                yield
        results.append((solution, phibar))

    chunk_len = snapshots // CHUNKS
    results = [[] for _ in range(CHUNKS)]
    runs = [
        run_chunk(right_side[k * chunk_len:(k + 1) * chunk_len], results[k])
        for k in range(CHUNKS)
    ]
    active = list(runs)
    while active:
        still = []
        for run in active:
            try:
                next(run)
                still.append(run)
            except StopIteration:
                pass
        active = still
    solution = jnp.concatenate([r[0][0] for r in results], axis=0)
    phibar = jnp.concatenate([r[0][1] for r in results], axis=0)
    share_len = solution.shape[1] // row_count
    solution = lax.dynamic_slice_in_dim(solution, lax.axis_index("row") * share_len, share_len, 1)
    return (solution.reshape(snapshots, 1, solution.shape[1]), phibar)


def solution(mesh):
    placed = (
        P(None, "row"),
        P(("row", "col"), None, None),
        P(("row", "col"), None),
        P(("row", "col")),
        P(("row", "col")),
    )
    return jax.shard_map(
        per_device,
        mesh=mesh,
        in_specs=placed,
        out_specs=(P(None, "col", "row"), P()),
        check_vma=False,
    )
```

```python
import jax
import jax.numpy as jnp
from jax import lax
from jax.sharding import PartitionSpec as P

TC = 32
ITERS = 4
CHUNKS = 2


EPSILON = 1e-06


def partner_pairs(count, distance):
    return [(i, i ^ distance) for i in range(count)]


def is_power_of_two(count):
    return count & (count - 1) == 0


def small_sum(value, axis):
    count = lax.axis_size(axis)
    if not is_power_of_two(count):
        return lax.psum(value, axis)
    distance = 1
    while distance < count:
        value = value + lax.ppermute(value, axis, partner_pairs(count, distance))
        distance *= 2
    return value


def big_sum(value, axis):
    count = lax.axis_size(axis)
    width = value.shape[-1]
    if not is_power_of_two(count) or width % (128 * count):
        return lax.psum(value, axis)
    index = lax.axis_index(axis)
    distances = []
    distance = 1
    while distance < count:
        distances.append(distance)
        distance *= 2
    held = value
    last = distances.pop()
    for distance in distances:
        half = held.shape[-1] // 2
        upper = (index // distance) % 2
        keep = lax.dynamic_slice_in_dim(held, upper * half, half, held.ndim - 1)
        give = lax.dynamic_slice_in_dim(held, (1 - upper) * half, half, held.ndim - 1)
        held = keep + lax.ppermute(give, axis, partner_pairs(count, distance))
    held = held + lax.ppermute(held, axis, partner_pairs(count, last))
    for distance in reversed(distances):
        upper = (index // distance) % 2
        other = lax.ppermute(held, axis, partner_pairs(count, distance))
        held = jnp.where(
            upper == 1,
            jnp.concatenate([other, held], axis=-1),
            jnp.concatenate([held, other], axis=-1),
        )
    return held


def gather_tiles(vector_bf, indices, block_size):
    snapshots, extent = vector_bf.shape
    vector_tiles = vector_bf.reshape(snapshots, extent // block_size, block_size)
    return jnp.take(vector_tiles, indices, axis=1)


def place_terms(weighted, indices, n_out):
    snapshots, number, block_size = weighted.shape
    onehot = (indices[:, None] == jnp.arange(n_out, dtype=jnp.int32)[None, :]).astype(jnp.float32)
    summed = jnp.einsum("ksi,st->kti", weighted, onehot, precision=lax.Precision.HIGHEST)
    return summed.reshape(snapshots, n_out * block_size)


def forward_terms(vector_bf, blocks, row_index, col_index, n_out):
    picked = gather_tiles(vector_bf, col_index, blocks.shape[1])
    weighted = jnp.einsum("sij,ksj->ksi", blocks, picked, preferred_element_type=jnp.float32)
    return place_terms(weighted, row_index, n_out)


def backward_terms(vector_bf, blocks, row_index, col_index, n_out):
    picked = gather_tiles(vector_bf, row_index, blocks.shape[1])
    weighted = jnp.einsum("sji,ksj->ksi", blocks, picked, preferred_element_type=jnp.float32)
    return place_terms(weighted, col_index, n_out)


def per_device(right_side, blocks, targets, tile_rows, tile_cols):
    col_count = lax.axis_size("col")
    row_count = lax.axis_size("row")
    block_size = blocks.shape[1]
    snapshots = right_side.shape[0]
    row_tiles = right_side.shape[1] // block_size
    own_count = blocks.shape[0]
    capacity = 2 * own_count // col_count
    target = targets[:, 0]
    matches = (target[:, None] == jnp.arange(col_count, dtype=jnp.int32)[None, :]).astype(jnp.int32)
    before = jnp.cumsum(matches, axis=0) - matches
    slot_index = target * capacity + jnp.sum(before * matches, axis=1)
    outgoing = (
        jnp.zeros((col_count * capacity, block_size, block_size), blocks.dtype)
        .at[slot_index]
        .set(blocks)
    )
    places = (
        jnp.zeros((col_count * capacity, 2), jnp.int32)
        .at[slot_index]
        .set(jnp.stack([tile_rows, tile_cols], axis=1))
    )
    arrived, arrived_places = (
        lax.all_to_all(
            outgoing.reshape(col_count, capacity, block_size, block_size),
            "col",
            split_axis=0,
            concat_axis=0,
            tiled=True,
        ),
        lax.all_to_all(
            places.reshape(col_count, capacity, 2), "col", split_axis=0, concat_axis=0, tiled=True
        ),
    )
    work_blocks = arrived.reshape(col_count * capacity, block_size, block_size)
    flat_places = arrived_places.reshape(col_count * capacity, 2)
    work_rows = flat_places[:, 0]
    work_cols = flat_places[:, 1]

    def backward(left_bf):
        return backward_terms(left_bf, work_blocks, work_rows, work_cols, TC)

    def sum_right(partial_value):
        return big_sum(partial_value, "row")

    def finish_left(unscaled, need_form):
        squares = jnp.sum(unscaled * unscaled, axis=1)
        total = small_sum(squares, "row")
        beta_norm = jnp.sqrt(total + EPSILON)
        scaled = unscaled / beta_norm[:, None]
        rounded = None
        if need_form:
            rounded = scaled.astype(jnp.bfloat16)
        return (beta_norm, scaled, rounded)

    def finish_right(unscaled):
        squares = jnp.sum(unscaled * unscaled, axis=1)
        total = small_sum(squares, "col")
        alpha_norm = jnp.sqrt(total + EPSILON)
        scaled = unscaled / alpha_norm[:, None]
        rounded = scaled.astype(jnp.bfloat16)
        return (alpha_norm, scaled, rounded)

    def run_chunk(side, results):
        beta_norm, left_vec, left_bf = finish_left(side, True)
        yield
        alpha_norm, right_vec, right_bf = finish_right(sum_right(backward(left_bf)))
        yield
        search = right_vec
        solution = jnp.zeros_like(right_vec)
        phibar = beta_norm
        rhobar = alpha_norm
        for iteration in range(ITERS):
            last_turn = iteration + 1 == ITERS
            unscaled = (
                big_sum(forward_terms(right_bf, work_blocks, work_rows, work_cols, row_tiles), "col")
                - alpha_norm[:, None] * left_vec
            )
            beta_norm, left_vec, left_bf = finish_left(unscaled, not last_turn)
            rho_value = jnp.sqrt(rhobar * rhobar + beta_norm * beta_norm)
            cosine = rhobar / rho_value
            sine_value = beta_norm / rho_value
            phi_value = cosine * phibar
            phibar = sine_value * phibar
            solution = solution + (phi_value / rho_value)[:, None] * search
            yield
            if not last_turn:
                unscaled = sum_right(backward(left_bf)) - beta_norm[:, None] * right_vec
                alpha_norm, right_vec, right_bf = finish_right(unscaled)
                theta_value = sine_value * alpha_norm
                rhobar = -cosine * alpha_norm
                search = right_vec - (theta_value / rho_value)[:, None] * search
                yield
        results.append((solution, phibar))

    chunk_len = snapshots // CHUNKS
    results = [[] for _ in range(CHUNKS)]
    runs = [
        run_chunk(right_side[k * chunk_len:(k + 1) * chunk_len], results[k])
        for k in range(CHUNKS)
    ]
    active = list(runs)
    while active:
        still = []
        for run in active:
            try:
                next(run)
                still.append(run)
            except StopIteration:
                pass
        active = still
    solution = jnp.concatenate([r[0][0] for r in results], axis=0)
    phibar = jnp.concatenate([r[0][1] for r in results], axis=0)
    share_len = solution.shape[1] // row_count
    solution = lax.dynamic_slice_in_dim(solution, lax.axis_index("row") * share_len, share_len, 1)
    return (solution.reshape(snapshots, 1, solution.shape[1]), phibar)


def solution(mesh):
    placed = (
        P(None, "row"),
        P(("row", "col"), None, None),
        P(("row", "col"), None),
        P(("row", "col")),
        P(("row", "col")),
    )
    return jax.shard_map(
        per_device,
        mesh=mesh,
        in_specs=placed,
        out_specs=(P(None, "col", "row"), P()),
        check_vma=False,
    )
```

```python
import jax
import jax.numpy as jnp
from jax import lax
from jax.sharding import PartitionSpec as P

TC = 32
ITERS = 4
CHUNKS = 2


EPSILON = 1e-06


def partner_pairs(count, distance):
    return [(i, i ^ distance) for i in range(count)]


def is_power_of_two(count):
    return count & (count - 1) == 0


def small_sum(value, axis):
    count = lax.axis_size(axis)
    if not is_power_of_two(count):
        return lax.psum(value, axis)
    distance = 1
    while distance < count:
        value = value + lax.ppermute(value, axis, partner_pairs(count, distance))
        distance *= 2
    return value


def big_sum(value, axis):
    count = lax.axis_size(axis)
    width = value.shape[-1]
    if not is_power_of_two(count) or width % (128 * count):
        return lax.psum(value, axis)
    index = lax.axis_index(axis)
    distances = []
    distance = 1
    while distance < count:
        distances.append(distance)
        distance *= 2
    held = value
    last = distances.pop()
    for distance in distances:
        half = held.shape[-1] // 2
        upper = (index // distance) % 2
        keep = lax.dynamic_slice_in_dim(held, upper * half, half, held.ndim - 1)
        give = lax.dynamic_slice_in_dim(held, (1 - upper) * half, half, held.ndim - 1)
        held = keep + lax.ppermute(give, axis, partner_pairs(count, distance))
    held = held + lax.ppermute(held, axis, partner_pairs(count, last))
    for distance in reversed(distances):
        upper = (index // distance) % 2
        other = lax.ppermute(held, axis, partner_pairs(count, distance))
        held = jnp.where(
            upper == 1,
            jnp.concatenate([other, held], axis=-1),
            jnp.concatenate([held, other], axis=-1),
        )
    return held


def gather_tiles(vector_bf, indices, block_size):
    snapshots, extent = vector_bf.shape
    vector_tiles = vector_bf.reshape(snapshots, extent // block_size, block_size)
    return jnp.take(vector_tiles, indices, axis=1)


def place_terms(weighted, indices, n_out):
    snapshots, number, block_size = weighted.shape
    onehot = (indices[:, None] == jnp.arange(n_out, dtype=jnp.int32)[None, :]).astype(jnp.float32)
    summed = jnp.einsum("ksi,st->kti", weighted, onehot, precision=lax.Precision.HIGH)
    return summed.reshape(snapshots, n_out * block_size)


def forward_terms(vector_bf, blocks, row_index, col_index, n_out):
    picked = gather_tiles(vector_bf, col_index, blocks.shape[1])
    weighted = jnp.einsum("sij,ksj->ksi", blocks, picked, preferred_element_type=jnp.float32)
    return place_terms(weighted, row_index, n_out)


def backward_terms(vector_bf, blocks, row_index, col_index, n_out):
    picked = gather_tiles(vector_bf, row_index, blocks.shape[1])
    weighted = jnp.einsum("sji,ksj->ksi", blocks, picked, preferred_element_type=jnp.float32)
    return place_terms(weighted, col_index, n_out)


def per_device(right_side, blocks, targets, tile_rows, tile_cols):
    col_count = lax.axis_size("col")
    row_count = lax.axis_size("row")
    block_size = blocks.shape[1]
    snapshots = right_side.shape[0]
    row_tiles = right_side.shape[1] // block_size
    own_count = blocks.shape[0]
    capacity = 2 * own_count // col_count
    target = targets[:, 0]
    matches = (target[:, None] == jnp.arange(col_count, dtype=jnp.int32)[None, :]).astype(jnp.int32)
    before = jnp.cumsum(matches, axis=0) - matches
    slot_index = target * capacity + jnp.sum(before * matches, axis=1)
    outgoing = (
        jnp.zeros((col_count * capacity, block_size, block_size), blocks.dtype)
        .at[slot_index]
        .set(blocks)
    )
    places = (
        jnp.zeros((col_count * capacity, 2), jnp.int32)
        .at[slot_index]
        .set(jnp.stack([tile_rows, tile_cols], axis=1))
    )
    arrived, arrived_places = (
        lax.all_to_all(
            outgoing.reshape(col_count, capacity, block_size, block_size),
            "col",
            split_axis=0,
            concat_axis=0,
            tiled=True,
        ),
        lax.all_to_all(
            places.reshape(col_count, capacity, 2), "col", split_axis=0, concat_axis=0, tiled=True
        ),
    )
    work_blocks = arrived.reshape(col_count * capacity, block_size, block_size)
    flat_places = arrived_places.reshape(col_count * capacity, 2)
    work_rows = flat_places[:, 0]
    work_cols = flat_places[:, 1]

    def backward(left_bf):
        return backward_terms(left_bf, work_blocks, work_rows, work_cols, TC)

    def sum_right(partial_value):
        return big_sum(partial_value, "row")

    def finish_left(unscaled, need_form):
        squares = jnp.sum(unscaled * unscaled, axis=1)
        total = small_sum(squares, "row")
        beta_norm = jnp.sqrt(total + EPSILON)
        scaled = unscaled / beta_norm[:, None]
        rounded = None
        if need_form:
            rounded = scaled.astype(jnp.bfloat16)
        return (beta_norm, scaled, rounded)

    def finish_right(unscaled):
        squares = jnp.sum(unscaled * unscaled, axis=1)
        total = small_sum(squares, "col")
        alpha_norm = jnp.sqrt(total + EPSILON)
        scaled = unscaled / alpha_norm[:, None]
        rounded = scaled.astype(jnp.bfloat16)
        return (alpha_norm, scaled, rounded)

    def run_chunk(side, results):
        beta_norm, left_vec, left_bf = finish_left(side, True)
        yield
        alpha_norm, right_vec, right_bf = finish_right(sum_right(backward(left_bf)))
        yield
        search = right_vec
        solution = jnp.zeros_like(right_vec)
        phibar = beta_norm
        rhobar = alpha_norm
        for iteration in range(ITERS):
            last_turn = iteration + 1 == ITERS
            unscaled = (
                big_sum(forward_terms(right_bf, work_blocks, work_rows, work_cols, row_tiles), "col")
                - alpha_norm[:, None] * left_vec
            )
            beta_norm, left_vec, left_bf = finish_left(unscaled, not last_turn)
            rho_value = jnp.sqrt(rhobar * rhobar + beta_norm * beta_norm)
            cosine = rhobar / rho_value
            sine_value = beta_norm / rho_value
            phi_value = cosine * phibar
            phibar = sine_value * phibar
            solution = solution + (phi_value / rho_value)[:, None] * search
            yield
            if not last_turn:
                unscaled = sum_right(backward(left_bf)) - beta_norm[:, None] * right_vec
                alpha_norm, right_vec, right_bf = finish_right(unscaled)
                theta_value = sine_value * alpha_norm
                rhobar = -cosine * alpha_norm
                search = right_vec - (theta_value / rho_value)[:, None] * search
                yield
        results.append((solution, phibar))

    chunk_len = snapshots // CHUNKS
    results = [[] for _ in range(CHUNKS)]
    runs = [
        run_chunk(right_side[k * chunk_len:(k + 1) * chunk_len], results[k])
        for k in range(CHUNKS)
    ]
    active = list(runs)
    while active:
        still = []
        for run in active:
            try:
                next(run)
                still.append(run)
            except StopIteration:
                pass
        active = still
    solution = jnp.concatenate([r[0][0] for r in results], axis=0)
    phibar = jnp.concatenate([r[0][1] for r in results], axis=0)
    share_len = solution.shape[1] // row_count
    solution = lax.dynamic_slice_in_dim(solution, lax.axis_index("row") * share_len, share_len, 1)
    return (solution.reshape(snapshots, 1, solution.shape[1]), phibar)


def solution(mesh):
    placed = (
        P(None, "row"),
        P(("row", "col"), None, None),
        P(("row", "col"), None),
        P(("row", "col")),
        P(("row", "col")),
    )
    return jax.shard_map(
        per_device,
        mesh=mesh,
        in_specs=placed,
        out_specs=(P(None, "col", "row"), P()),
        check_vma=False,
    )
```

```python
import jax
import jax.numpy as jnp
from jax import lax
from jax.sharding import PartitionSpec as P

TC = 32
ITERS = 4
CHUNKS = 2


EPSILON = 1e-06


def partner_pairs(count, distance):
    return [(i, i ^ distance) for i in range(count)]


def is_power_of_two(count):
    return count & (count - 1) == 0


def small_sum(value, axis):
    count = lax.axis_size(axis)
    if not is_power_of_two(count):
        return lax.psum(value, axis)
    lanes = jnp.split(value, CHUNKS, axis=0)
    distance = 1
    while distance < count:
        lanes = [lane + lax.ppermute(lane, axis, partner_pairs(count, distance)) for lane in lanes]
        distance *= 2
    return jnp.concatenate(lanes, axis=0)


def big_sum(value, axis):
    count = lax.axis_size(axis)
    width = value.shape[-1]
    if not is_power_of_two(count) or width % (128 * count):
        return lax.psum(value, axis)
    index = lax.axis_index(axis)
    distances = []
    distance = 1
    while distance < count:
        distances.append(distance)
        distance *= 2
    lanes = jnp.split(value, CHUNKS, axis=0)
    last = distances.pop()
    for distance in distances:
        upper = (index // distance) % 2
        moved = []
        for held in lanes:
            half = held.shape[-1] // 2
            keep = lax.dynamic_slice_in_dim(held, upper * half, half, held.ndim - 1)
            give = lax.dynamic_slice_in_dim(held, (1 - upper) * half, half, held.ndim - 1)
            moved.append(keep + lax.ppermute(give, axis, partner_pairs(count, distance)))
        lanes = moved
    lanes = [held + lax.ppermute(held, axis, partner_pairs(count, last)) for held in lanes]
    for distance in reversed(distances):
        upper = (index // distance) % 2
        moved = []
        for held in lanes:
            other = lax.ppermute(held, axis, partner_pairs(count, distance))
            moved.append(jnp.where(
                upper == 1,
                jnp.concatenate([other, held], axis=-1),
                jnp.concatenate([held, other], axis=-1),
            ))
        lanes = moved
    return jnp.concatenate(lanes, axis=0)


def gather_tiles(vector_bf, indices, block_size):
    snapshots, extent = vector_bf.shape
    vector_tiles = vector_bf.reshape(snapshots, extent // block_size, block_size)
    return jnp.take(vector_tiles, indices, axis=1)


def place_terms(weighted, indices, n_out):
    snapshots, number, block_size = weighted.shape
    onehot = (indices[:, None] == jnp.arange(n_out, dtype=jnp.int32)[None, :]).astype(jnp.float32)
    summed = jnp.einsum("ksi,st->kti", weighted, onehot, precision=lax.Precision.HIGH)
    return summed.reshape(snapshots, n_out * block_size)


def forward_terms(vector_bf, blocks, row_index, col_index, n_out):
    picked = gather_tiles(vector_bf, col_index, blocks.shape[1])
    weighted = jnp.einsum("sij,ksj->ksi", blocks, picked, preferred_element_type=jnp.float32)
    return place_terms(weighted, row_index, n_out)


def backward_terms(vector_bf, blocks, row_index, col_index, n_out):
    picked = gather_tiles(vector_bf, row_index, blocks.shape[1])
    weighted = jnp.einsum("sji,ksj->ksi", blocks, picked, preferred_element_type=jnp.float32)
    return place_terms(weighted, col_index, n_out)


def per_device(right_side, blocks, targets, tile_rows, tile_cols):
    col_count = lax.axis_size("col")
    row_count = lax.axis_size("row")
    block_size = blocks.shape[1]
    snapshots = right_side.shape[0]
    row_tiles = right_side.shape[1] // block_size
    own_count = blocks.shape[0]
    capacity = 2 * own_count // col_count
    target = targets[:, 0]
    matches = (target[:, None] == jnp.arange(col_count, dtype=jnp.int32)[None, :]).astype(jnp.int32)
    before = jnp.cumsum(matches, axis=0) - matches
    slot_index = target * capacity + jnp.sum(before * matches, axis=1)
    outgoing = (
        jnp.zeros((col_count * capacity, block_size, block_size), blocks.dtype)
        .at[slot_index]
        .set(blocks)
    )
    places = (
        jnp.zeros((col_count * capacity, 2), jnp.int32)
        .at[slot_index]
        .set(jnp.stack([tile_rows, tile_cols], axis=1))
    )
    arrived, arrived_places = (
        lax.all_to_all(
            outgoing.reshape(col_count, capacity, block_size, block_size),
            "col",
            split_axis=0,
            concat_axis=0,
            tiled=True,
        ),
        lax.all_to_all(
            places.reshape(col_count, capacity, 2), "col", split_axis=0, concat_axis=0, tiled=True
        ),
    )
    work_blocks = arrived.reshape(col_count * capacity, block_size, block_size)
    flat_places = arrived_places.reshape(col_count * capacity, 2)
    work_rows = flat_places[:, 0]
    work_cols = flat_places[:, 1]

    def backward(left_bf):
        return backward_terms(left_bf, work_blocks, work_rows, work_cols, TC)

    def sum_right(partial_value):
        return big_sum(partial_value, "row")

    def finish_left(unscaled, need_form):
        squares = jnp.sum(unscaled * unscaled, axis=1)
        total = small_sum(squares, "row")
        beta_norm = jnp.sqrt(total + EPSILON)
        scaled = unscaled / beta_norm[:, None]
        rounded = None
        if need_form:
            rounded = scaled.astype(jnp.bfloat16)
        return (beta_norm, scaled, rounded)

    def finish_right(unscaled):
        squares = jnp.sum(unscaled * unscaled, axis=1)
        total = small_sum(squares, "col")
        alpha_norm = jnp.sqrt(total + EPSILON)
        scaled = unscaled / alpha_norm[:, None]
        rounded = scaled.astype(jnp.bfloat16)
        return (alpha_norm, scaled, rounded)

    beta_norm, left_vec, left_bf = finish_left(right_side, True)
    alpha_norm, right_vec, right_bf = finish_right(sum_right(backward(left_bf)))
    search = right_vec
    solution = jnp.zeros_like(right_vec)
    phibar = beta_norm
    rhobar = alpha_norm
    for iteration in range(ITERS):
        last_turn = iteration + 1 == ITERS
        unscaled = (
            big_sum(forward_terms(right_bf, work_blocks, work_rows, work_cols, row_tiles), "col")
            - alpha_norm[:, None] * left_vec
        )
        beta_norm, left_vec, left_bf = finish_left(unscaled, not last_turn)
        rho_value = jnp.sqrt(rhobar * rhobar + beta_norm * beta_norm)
        cosine = rhobar / rho_value
        sine_value = beta_norm / rho_value
        phi_value = cosine * phibar
        phibar = sine_value * phibar
        solution = solution + (phi_value / rho_value)[:, None] * search
        if not last_turn:
            unscaled = sum_right(backward(left_bf)) - beta_norm[:, None] * right_vec
            alpha_norm, right_vec, right_bf = finish_right(unscaled)
            theta_value = sine_value * alpha_norm
            rhobar = -cosine * alpha_norm
            search = right_vec - (theta_value / rho_value)[:, None] * search
    share_len = solution.shape[1] // row_count
    solution = lax.dynamic_slice_in_dim(solution, lax.axis_index("row") * share_len, share_len, 1)
    return (solution.reshape(snapshots, 1, solution.shape[1]), phibar)


def solution(mesh):
    placed = (
        P(None, "row"),
        P(("row", "col"), None, None),
        P(("row", "col"), None),
        P(("row", "col")),
        P(("row", "col")),
    )
    return jax.shard_map(
        per_device,
        mesh=mesh,
        in_specs=placed,
        out_specs=(P(None, "col", "row"), P()),
        check_vma=False,
    )
```

```python
import jax
import jax.numpy as jnp
from jax import lax
from jax.sharding import PartitionSpec as P

TC = 32
ITERS = 4
CHUNKS = 4


EPSILON = 1e-06


def partner_pairs(count, distance):
    return [(i, i ^ distance) for i in range(count)]


def is_power_of_two(count):
    return count & (count - 1) == 0


def small_sum(value, axis):
    count = lax.axis_size(axis)
    if not is_power_of_two(count):
        return lax.psum(value, axis)
    lanes = jnp.split(value, CHUNKS, axis=0)
    distance = 1
    while distance < count:
        lanes = [lane + lax.ppermute(lane, axis, partner_pairs(count, distance)) for lane in lanes]
        distance *= 2
    return jnp.concatenate(lanes, axis=0)


def big_sum(value, axis):
    count = lax.axis_size(axis)
    width = value.shape[-1]
    if not is_power_of_two(count) or width % (128 * count):
        return lax.psum(value, axis)
    index = lax.axis_index(axis)
    distances = []
    distance = 1
    while distance < count:
        distances.append(distance)
        distance *= 2
    lanes = jnp.split(value, CHUNKS, axis=0)
    last = distances.pop()
    for distance in distances:
        upper = (index // distance) % 2
        moved = []
        for held in lanes:
            half = held.shape[-1] // 2
            keep = lax.dynamic_slice_in_dim(held, upper * half, half, held.ndim - 1)
            give = lax.dynamic_slice_in_dim(held, (1 - upper) * half, half, held.ndim - 1)
            moved.append(keep + lax.ppermute(give, axis, partner_pairs(count, distance)))
        lanes = moved
    lanes = [held + lax.ppermute(held, axis, partner_pairs(count, last)) for held in lanes]
    for distance in reversed(distances):
        upper = (index // distance) % 2
        moved = []
        for held in lanes:
            other = lax.ppermute(held, axis, partner_pairs(count, distance))
            moved.append(jnp.where(
                upper == 1,
                jnp.concatenate([other, held], axis=-1),
                jnp.concatenate([held, other], axis=-1),
            ))
        lanes = moved
    return jnp.concatenate(lanes, axis=0)


def gather_tiles(vector_bf, indices, block_size):
    snapshots, extent = vector_bf.shape
    vector_tiles = vector_bf.reshape(snapshots, extent // block_size, block_size)
    return jnp.take(vector_tiles, indices, axis=1)


def place_terms(weighted, indices, n_out):
    snapshots, number, block_size = weighted.shape
    onehot = (indices[:, None] == jnp.arange(n_out, dtype=jnp.int32)[None, :]).astype(jnp.float32)
    summed = jnp.einsum("ksi,st->kti", weighted, onehot, precision=lax.Precision.HIGH)
    return summed.reshape(snapshots, n_out * block_size)


def forward_terms(vector_bf, blocks, row_index, col_index, n_out):
    picked = gather_tiles(vector_bf, col_index, blocks.shape[1])
    weighted = jnp.einsum("sij,ksj->ksi", blocks, picked, preferred_element_type=jnp.float32)
    return place_terms(weighted, row_index, n_out)


def backward_terms(vector_bf, blocks, row_index, col_index, n_out):
    picked = gather_tiles(vector_bf, row_index, blocks.shape[1])
    weighted = jnp.einsum("sji,ksj->ksi", blocks, picked, preferred_element_type=jnp.float32)
    return place_terms(weighted, col_index, n_out)


def per_device(right_side, blocks, targets, tile_rows, tile_cols):
    col_count = lax.axis_size("col")
    row_count = lax.axis_size("row")
    block_size = blocks.shape[1]
    snapshots = right_side.shape[0]
    row_tiles = right_side.shape[1] // block_size
    own_count = blocks.shape[0]
    capacity = 2 * own_count // col_count
    target = targets[:, 0]
    matches = (target[:, None] == jnp.arange(col_count, dtype=jnp.int32)[None, :]).astype(jnp.int32)
    before = jnp.cumsum(matches, axis=0) - matches
    slot_index = target * capacity + jnp.sum(before * matches, axis=1)
    outgoing = (
        jnp.zeros((col_count * capacity, block_size, block_size), blocks.dtype)
        .at[slot_index]
        .set(blocks)
    )
    places = (
        jnp.zeros((col_count * capacity, 2), jnp.int32)
        .at[slot_index]
        .set(jnp.stack([tile_rows, tile_cols], axis=1))
    )
    arrived, arrived_places = (
        lax.all_to_all(
            outgoing.reshape(col_count, capacity, block_size, block_size),
            "col",
            split_axis=0,
            concat_axis=0,
            tiled=True,
        ),
        lax.all_to_all(
            places.reshape(col_count, capacity, 2), "col", split_axis=0, concat_axis=0, tiled=True
        ),
    )
    work_blocks = arrived.reshape(col_count * capacity, block_size, block_size)
    flat_places = arrived_places.reshape(col_count * capacity, 2)
    work_rows = flat_places[:, 0]
    work_cols = flat_places[:, 1]

    def backward(left_bf):
        return backward_terms(left_bf, work_blocks, work_rows, work_cols, TC)

    def sum_right(partial_value):
        return big_sum(partial_value, "row")

    def finish_left(unscaled, need_form):
        squares = jnp.sum(unscaled * unscaled, axis=1)
        total = small_sum(squares, "row")
        beta_norm = jnp.sqrt(total + EPSILON)
        scaled = unscaled / beta_norm[:, None]
        rounded = None
        if need_form:
            rounded = scaled.astype(jnp.bfloat16)
        return (beta_norm, scaled, rounded)

    def finish_right(unscaled):
        squares = jnp.sum(unscaled * unscaled, axis=1)
        total = small_sum(squares, "col")
        alpha_norm = jnp.sqrt(total + EPSILON)
        scaled = unscaled / alpha_norm[:, None]
        rounded = scaled.astype(jnp.bfloat16)
        return (alpha_norm, scaled, rounded)

    beta_norm, left_vec, left_bf = finish_left(right_side, True)
    alpha_norm, right_vec, right_bf = finish_right(sum_right(backward(left_bf)))
    search = right_vec
    solution = jnp.zeros_like(right_vec)
    phibar = beta_norm
    rhobar = alpha_norm
    for iteration in range(ITERS):
        last_turn = iteration + 1 == ITERS
        unscaled = (
            big_sum(forward_terms(right_bf, work_blocks, work_rows, work_cols, row_tiles), "col")
            - alpha_norm[:, None] * left_vec
        )
        beta_norm, left_vec, left_bf = finish_left(unscaled, not last_turn)
        rho_value = jnp.sqrt(rhobar * rhobar + beta_norm * beta_norm)
        cosine = rhobar / rho_value
        sine_value = beta_norm / rho_value
        phi_value = cosine * phibar
        phibar = sine_value * phibar
        solution = solution + (phi_value / rho_value)[:, None] * search
        if not last_turn:
            unscaled = sum_right(backward(left_bf)) - beta_norm[:, None] * right_vec
            alpha_norm, right_vec, right_bf = finish_right(unscaled)
            theta_value = sine_value * alpha_norm
            rhobar = -cosine * alpha_norm
            search = right_vec - (theta_value / rho_value)[:, None] * search
    share_len = solution.shape[1] // row_count
    solution = lax.dynamic_slice_in_dim(solution, lax.axis_index("row") * share_len, share_len, 1)
    return (solution.reshape(snapshots, 1, solution.shape[1]), phibar)


def solution(mesh):
    placed = (
        P(None, "row"),
        P(("row", "col"), None, None),
        P(("row", "col"), None),
        P(("row", "col")),
        P(("row", "col")),
    )
    return jax.shard_map(
        per_device,
        mesh=mesh,
        in_specs=placed,
        out_specs=(P(None, "col", "row"), P()),
        check_vma=False,
    )
```

```python
import jax
import jax.numpy as jnp
from jax import lax
from jax.sharding import PartitionSpec as P

TC = 32
ITERS = 4
CHUNKS = 2


EPSILON = 1e-06


def partner_pairs(count, distance):
    return [(i, i ^ distance) for i in range(count)]


def is_power_of_two(count):
    return count & (count - 1) == 0


def small_sum(value, axis):
    count = lax.axis_size(axis)
    if not is_power_of_two(count):
        return lax.psum(value, axis)
    distance = 1
    while distance < count:
        value = value + lax.ppermute(value, axis, partner_pairs(count, distance))
        distance *= 2
    return value


def big_sum(value, axis):
    count = lax.axis_size(axis)
    width = value.shape[-1]
    if not is_power_of_two(count) or width % (128 * count):
        return lax.psum(value, axis)
    index = lax.axis_index(axis)
    distances = []
    distance = 1
    while distance < count:
        distances.append(distance)
        distance *= 2
    lanes = jnp.split(value, CHUNKS, axis=0)
    last = distances.pop()
    for distance in distances:
        upper = (index // distance) % 2
        moved = []
        for held in lanes:
            half = held.shape[-1] // 2
            keep = lax.dynamic_slice_in_dim(held, upper * half, half, held.ndim - 1)
            give = lax.dynamic_slice_in_dim(held, (1 - upper) * half, half, held.ndim - 1)
            moved.append(keep + lax.ppermute(give, axis, partner_pairs(count, distance)))
        lanes = moved
    lanes = [held + lax.ppermute(held, axis, partner_pairs(count, last)) for held in lanes]
    for distance in reversed(distances):
        upper = (index // distance) % 2
        moved = []
        for held in lanes:
            other = lax.ppermute(held, axis, partner_pairs(count, distance))
            moved.append(jnp.where(
                upper == 1,
                jnp.concatenate([other, held], axis=-1),
                jnp.concatenate([held, other], axis=-1),
            ))
        lanes = moved
    return jnp.concatenate(lanes, axis=0)


def gather_tiles(vector_bf, indices, block_size):
    snapshots, extent = vector_bf.shape
    vector_tiles = vector_bf.reshape(snapshots, extent // block_size, block_size)
    return jnp.take(vector_tiles, indices, axis=1)


def place_terms(weighted, indices, n_out):
    snapshots, number, block_size = weighted.shape
    onehot = (indices[:, None] == jnp.arange(n_out, dtype=jnp.int32)[None, :]).astype(jnp.float32)
    summed = jnp.einsum("ksi,st->kti", weighted, onehot, precision=lax.Precision.HIGH)
    return summed.reshape(snapshots, n_out * block_size)


def forward_terms(vector_bf, blocks, row_index, col_index, n_out):
    picked = gather_tiles(vector_bf, col_index, blocks.shape[1])
    weighted = jnp.einsum("sij,ksj->ksi", blocks, picked, preferred_element_type=jnp.float32)
    return place_terms(weighted, row_index, n_out)


def backward_terms(vector_bf, blocks, row_index, col_index, n_out):
    picked = gather_tiles(vector_bf, row_index, blocks.shape[1])
    weighted = jnp.einsum("sji,ksj->ksi", blocks, picked, preferred_element_type=jnp.float32)
    return place_terms(weighted, col_index, n_out)


def per_device(right_side, blocks, targets, tile_rows, tile_cols):
    col_count = lax.axis_size("col")
    row_count = lax.axis_size("row")
    block_size = blocks.shape[1]
    snapshots = right_side.shape[0]
    row_tiles = right_side.shape[1] // block_size
    own_count = blocks.shape[0]
    capacity = 2 * own_count // col_count
    target = targets[:, 0]
    matches = (target[:, None] == jnp.arange(col_count, dtype=jnp.int32)[None, :]).astype(jnp.int32)
    before = jnp.cumsum(matches, axis=0) - matches
    slot_index = target * capacity + jnp.sum(before * matches, axis=1)
    outgoing = (
        jnp.zeros((col_count * capacity, block_size, block_size), blocks.dtype)
        .at[slot_index]
        .set(blocks)
    )
    places = (
        jnp.zeros((col_count * capacity, 2), jnp.int32)
        .at[slot_index]
        .set(jnp.stack([tile_rows, tile_cols], axis=1))
    )
    arrived, arrived_places = (
        lax.all_to_all(
            outgoing.reshape(col_count, capacity, block_size, block_size),
            "col",
            split_axis=0,
            concat_axis=0,
            tiled=True,
        ),
        lax.all_to_all(
            places.reshape(col_count, capacity, 2), "col", split_axis=0, concat_axis=0, tiled=True
        ),
    )
    work_blocks = arrived.reshape(col_count * capacity, block_size, block_size)
    flat_places = arrived_places.reshape(col_count * capacity, 2)
    work_rows = flat_places[:, 0]
    work_cols = flat_places[:, 1]

    def backward(left_bf):
        return backward_terms(left_bf, work_blocks, work_rows, work_cols, TC)

    def sum_right(partial_value):
        return big_sum(partial_value, "row")

    def finish_left(unscaled, need_form):
        squares = jnp.sum(unscaled * unscaled, axis=1)
        total = small_sum(squares, "row")
        beta_norm = jnp.sqrt(total + EPSILON)
        scaled = unscaled / beta_norm[:, None]
        rounded = None
        if need_form:
            rounded = scaled.astype(jnp.bfloat16)
        return (beta_norm, scaled, rounded)

    def finish_right(unscaled):
        squares = jnp.sum(unscaled * unscaled, axis=1)
        total = small_sum(squares, "col")
        alpha_norm = jnp.sqrt(total + EPSILON)
        scaled = unscaled / alpha_norm[:, None]
        rounded = scaled.astype(jnp.bfloat16)
        return (alpha_norm, scaled, rounded)

    beta_norm, left_vec, left_bf = finish_left(right_side, True)
    alpha_norm, right_vec, right_bf = finish_right(sum_right(backward(left_bf)))
    search = right_vec
    solution = jnp.zeros_like(right_vec)
    phibar = beta_norm
    rhobar = alpha_norm
    for iteration in range(ITERS):
        last_turn = iteration + 1 == ITERS
        unscaled = (
            big_sum(forward_terms(right_bf, work_blocks, work_rows, work_cols, row_tiles), "col")
            - alpha_norm[:, None] * left_vec
        )
        beta_norm, left_vec, left_bf = finish_left(unscaled, not last_turn)
        rho_value = jnp.sqrt(rhobar * rhobar + beta_norm * beta_norm)
        cosine = rhobar / rho_value
        sine_value = beta_norm / rho_value
        phi_value = cosine * phibar
        phibar = sine_value * phibar
        solution = solution + (phi_value / rho_value)[:, None] * search
        if not last_turn:
            unscaled = sum_right(backward(left_bf)) - beta_norm[:, None] * right_vec
            alpha_norm, right_vec, right_bf = finish_right(unscaled)
            theta_value = sine_value * alpha_norm
            rhobar = -cosine * alpha_norm
            search = right_vec - (theta_value / rho_value)[:, None] * search
    share_len = solution.shape[1] // row_count
    solution = lax.dynamic_slice_in_dim(solution, lax.axis_index("row") * share_len, share_len, 1)
    return (solution.reshape(snapshots, 1, solution.shape[1]), phibar)


def solution(mesh):
    placed = (
        P(None, "row"),
        P(("row", "col"), None, None),
        P(("row", "col"), None),
        P(("row", "col")),
        P(("row", "col")),
    )
    return jax.shard_map(
        per_device,
        mesh=mesh,
        in_specs=placed,
        out_specs=(P(None, "col", "row"), P()),
        check_vma=False,
    )
```

```python
import jax
import jax.numpy as jnp
from jax import lax
from jax.sharding import PartitionSpec as P

TC = 32
ITERS = 4
CHUNKS = 2


EPSILON = 1e-06


def partner_pairs(count, distance):
    return [(i, i ^ distance) for i in range(count)]


def is_power_of_two(count):
    return count & (count - 1) == 0


def small_sum(value, axis):
    count = lax.axis_size(axis)
    if not is_power_of_two(count):
        return lax.psum(value, axis)
    distance = 1
    while distance < count:
        value = value + lax.ppermute(value, axis, partner_pairs(count, distance))
        distance *= 2
    return value


def big_sum(value, axis, lane_count):
    count = lax.axis_size(axis)
    width = value.shape[-1]
    if not is_power_of_two(count) or width % (128 * count):
        return lax.psum(value, axis)
    index = lax.axis_index(axis)
    distances = []
    distance = 1
    while distance < count:
        distances.append(distance)
        distance *= 2
    lanes = jnp.split(value, lane_count, axis=0)
    last = distances.pop()
    for distance in distances:
        upper = (index // distance) % 2
        moved = []
        for held in lanes:
            half = held.shape[-1] // 2
            keep = lax.dynamic_slice_in_dim(held, upper * half, half, held.ndim - 1)
            give = lax.dynamic_slice_in_dim(held, (1 - upper) * half, half, held.ndim - 1)
            moved.append(keep + lax.ppermute(give, axis, partner_pairs(count, distance)))
        lanes = moved
    lanes = [held + lax.ppermute(held, axis, partner_pairs(count, last)) for held in lanes]
    for distance in reversed(distances):
        upper = (index // distance) % 2
        moved = []
        for held in lanes:
            other = lax.ppermute(held, axis, partner_pairs(count, distance))
            moved.append(jnp.where(
                upper == 1,
                jnp.concatenate([other, held], axis=-1),
                jnp.concatenate([held, other], axis=-1),
            ))
        lanes = moved
    return jnp.concatenate(lanes, axis=0)


def gather_tiles(vector_bf, indices, block_size):
    snapshots, extent = vector_bf.shape
    vector_tiles = vector_bf.reshape(snapshots, extent // block_size, block_size)
    return jnp.take(vector_tiles, indices, axis=1)


def place_terms(weighted, indices, n_out):
    snapshots, number, block_size = weighted.shape
    onehot = (indices[:, None] == jnp.arange(n_out, dtype=jnp.int32)[None, :]).astype(jnp.float32)
    summed = jnp.einsum("ksi,st->kti", weighted, onehot, precision=lax.Precision.HIGH)
    return summed.reshape(snapshots, n_out * block_size)


def forward_terms(vector_bf, blocks, row_index, col_index, n_out):
    picked = gather_tiles(vector_bf, col_index, blocks.shape[1])
    weighted = jnp.einsum("sij,ksj->ksi", blocks, picked, preferred_element_type=jnp.float32)
    return place_terms(weighted, row_index, n_out)


def backward_terms(vector_bf, blocks, row_index, col_index, n_out):
    picked = gather_tiles(vector_bf, row_index, blocks.shape[1])
    weighted = jnp.einsum("sji,ksj->ksi", blocks, picked, preferred_element_type=jnp.float32)
    return place_terms(weighted, col_index, n_out)


def per_device(right_side, blocks, targets, tile_rows, tile_cols):
    col_count = lax.axis_size("col")
    row_count = lax.axis_size("row")
    block_size = blocks.shape[1]
    snapshots = right_side.shape[0]
    row_tiles = right_side.shape[1] // block_size
    own_count = blocks.shape[0]
    capacity = 2 * own_count // col_count
    target = targets[:, 0]
    matches = (target[:, None] == jnp.arange(col_count, dtype=jnp.int32)[None, :]).astype(jnp.int32)
    before = jnp.cumsum(matches, axis=0) - matches
    slot_index = target * capacity + jnp.sum(before * matches, axis=1)
    outgoing = (
        jnp.zeros((col_count * capacity, block_size, block_size), blocks.dtype)
        .at[slot_index]
        .set(blocks)
    )
    places = (
        jnp.zeros((col_count * capacity, 2), jnp.int32)
        .at[slot_index]
        .set(jnp.stack([tile_rows, tile_cols], axis=1))
    )
    arrived, arrived_places = (
        lax.all_to_all(
            outgoing.reshape(col_count, capacity, block_size, block_size),
            "col",
            split_axis=0,
            concat_axis=0,
            tiled=True,
        ),
        lax.all_to_all(
            places.reshape(col_count, capacity, 2), "col", split_axis=0, concat_axis=0, tiled=True
        ),
    )
    work_blocks = arrived.reshape(col_count * capacity, block_size, block_size)
    flat_places = arrived_places.reshape(col_count * capacity, 2)
    work_rows = flat_places[:, 0]
    work_cols = flat_places[:, 1]

    def backward(left_bf):
        return backward_terms(left_bf, work_blocks, work_rows, work_cols, TC)

    def sum_right(partial_value):
        return big_sum(partial_value, "row", 1)

    def finish_left(unscaled, need_form):
        squares = jnp.sum(unscaled * unscaled, axis=1)
        total = small_sum(squares, "row")
        beta_norm = jnp.sqrt(total + EPSILON)
        scaled = unscaled / beta_norm[:, None]
        rounded = None
        if need_form:
            rounded = scaled.astype(jnp.bfloat16)
        return (beta_norm, scaled, rounded)

    def finish_right(unscaled):
        squares = jnp.sum(unscaled * unscaled, axis=1)
        total = small_sum(squares, "col")
        alpha_norm = jnp.sqrt(total + EPSILON)
        scaled = unscaled / alpha_norm[:, None]
        rounded = scaled.astype(jnp.bfloat16)
        return (alpha_norm, scaled, rounded)

    beta_norm, left_vec, left_bf = finish_left(right_side, True)
    alpha_norm, right_vec, right_bf = finish_right(sum_right(backward(left_bf)))
    search = right_vec
    solution = jnp.zeros_like(right_vec)
    phibar = beta_norm
    rhobar = alpha_norm
    for iteration in range(ITERS):
        last_turn = iteration + 1 == ITERS
        unscaled = (
            big_sum(forward_terms(right_bf, work_blocks, work_rows, work_cols, row_tiles), "col", CHUNKS)
            - alpha_norm[:, None] * left_vec
        )
        beta_norm, left_vec, left_bf = finish_left(unscaled, not last_turn)
        rho_value = jnp.sqrt(rhobar * rhobar + beta_norm * beta_norm)
        cosine = rhobar / rho_value
        sine_value = beta_norm / rho_value
        phi_value = cosine * phibar
        phibar = sine_value * phibar
        solution = solution + (phi_value / rho_value)[:, None] * search
        if not last_turn:
            unscaled = sum_right(backward(left_bf)) - beta_norm[:, None] * right_vec
            alpha_norm, right_vec, right_bf = finish_right(unscaled)
            theta_value = sine_value * alpha_norm
            rhobar = -cosine * alpha_norm
            search = right_vec - (theta_value / rho_value)[:, None] * search
    share_len = solution.shape[1] // row_count
    solution = lax.dynamic_slice_in_dim(solution, lax.axis_index("row") * share_len, share_len, 1)
    return (solution.reshape(snapshots, 1, solution.shape[1]), phibar)


def solution(mesh):
    placed = (
        P(None, "row"),
        P(("row", "col"), None, None),
        P(("row", "col"), None),
        P(("row", "col")),
        P(("row", "col")),
    )
    return jax.shard_map(
        per_device,
        mesh=mesh,
        in_specs=placed,
        out_specs=(P(None, "col", "row"), P()),
        check_vma=False,
    )
```

```python
import jax
import jax.numpy as jnp
from jax import lax
from jax.sharding import PartitionSpec as P

TC = 32
ITERS = 4
CHUNKS = 2


EPSILON = 1e-06


def partner_pairs(count, distance):
    return [(i, i ^ distance) for i in range(count)]


def is_power_of_two(count):
    return count & (count - 1) == 0


def small_sum(value, axis):
    count = lax.axis_size(axis)
    if not is_power_of_two(count):
        return lax.psum(value, axis)
    distance = 1
    while distance < count:
        value = value + lax.ppermute(value, axis, partner_pairs(count, distance))
        distance *= 2
    return value


def big_sum(value, axis):
    count = lax.axis_size(axis)
    width = value.shape[-1]
    if not is_power_of_two(count) or width % (128 * count):
        return lax.psum(value, axis)
    index = lax.axis_index(axis)
    distances = []
    distance = 1
    while distance < count:
        distances.append(distance)
        distance *= 2
    lanes = jnp.split(value, CHUNKS, axis=0)
    last = distances.pop()
    for distance in distances:
        upper = (index // distance) % 2
        moved = []
        for held in lanes:
            half = held.shape[-1] // 2
            keep = lax.dynamic_slice_in_dim(held, upper * half, half, held.ndim - 1)
            give = lax.dynamic_slice_in_dim(held, (1 - upper) * half, half, held.ndim - 1)
            moved.append(keep + lax.ppermute(give, axis, partner_pairs(count, distance)))
        lanes = moved
    lanes = [held + lax.ppermute(held, axis, partner_pairs(count, last)) for held in lanes]
    for distance in reversed(distances):
        upper = (index // distance) % 2
        moved = []
        for held in lanes:
            other = lax.ppermute(held, axis, partner_pairs(count, distance))
            moved.append(jnp.where(
                upper == 1,
                jnp.concatenate([other, held], axis=-1),
                jnp.concatenate([held, other], axis=-1),
            ))
        lanes = moved
    return jnp.concatenate(lanes, axis=0)


def gather_tiles(vector_bf, indices, block_size):
    snapshots, extent = vector_bf.shape
    vector_tiles = vector_bf.reshape(snapshots, extent // block_size, block_size)
    return jnp.take(vector_tiles, indices, axis=1)


def place_terms(weighted, indices, n_out):
    snapshots, number, block_size = weighted.shape
    onehot = (indices[:, None] == jnp.arange(n_out, dtype=jnp.int32)[None, :]).astype(jnp.float32)
    summed = jnp.einsum("ksi,st->kti", weighted, onehot, precision=lax.Precision.HIGH)
    return summed.reshape(snapshots, n_out * block_size)


def forward_terms(vector_bf, blocks, row_index, col_index, n_out):
    picked = gather_tiles(vector_bf, col_index, blocks.shape[1])
    weighted = jnp.einsum("sij,ksj->ksi", blocks, picked, preferred_element_type=jnp.float32)
    return place_terms(weighted, row_index, n_out)


def backward_terms(vector_bf, blocks, row_index, col_index, n_out):
    picked = gather_tiles(vector_bf, row_index, blocks.shape[1])
    weighted = jnp.einsum("sji,ksj->ksi", blocks, picked, preferred_element_type=jnp.float32)
    return place_terms(weighted, col_index, n_out)


def per_device(right_side, blocks, targets, tile_rows, tile_cols):
    col_count = lax.axis_size("col")
    row_count = lax.axis_size("row")
    block_size = blocks.shape[1]
    snapshots = right_side.shape[0]
    row_tiles = right_side.shape[1] // block_size
    own_count = blocks.shape[0]
    capacity = 2 * own_count // col_count
    target = targets[:, 0]
    slot_count = col_count * capacity
    matches = (target[:, None] == jnp.arange(col_count, dtype=jnp.int32)[None, :]).astype(jnp.int32)
    before = jnp.cumsum(matches, axis=0) - matches
    slot_index = target * capacity + jnp.sum(before * matches, axis=1)
    pick = slot_index[:, None] == jnp.arange(slot_count, dtype=jnp.int32)[None, :]
    source = jnp.sum(jnp.where(pick, jnp.arange(own_count, dtype=jnp.int32)[:, None], 0), axis=0)
    source = jnp.where(jnp.any(pick, axis=0), source, own_count)
    padded = jnp.concatenate([blocks, jnp.zeros((1, block_size, block_size), blocks.dtype)], axis=0)
    outgoing = jnp.take(padded, source, axis=0, mode="clip")
    padded_places = jnp.concatenate(
        [jnp.stack([tile_rows, tile_cols], axis=1), jnp.zeros((1, 2), jnp.int32)], axis=0
    )
    places = jnp.take(padded_places, source, axis=0, mode="clip")
    arrived, arrived_places = (
        lax.all_to_all(
            outgoing.reshape(col_count, capacity, block_size, block_size),
            "col",
            split_axis=0,
            concat_axis=0,
            tiled=True,
        ),
        lax.all_to_all(
            places.reshape(col_count, capacity, 2), "col", split_axis=0, concat_axis=0, tiled=True
        ),
    )
    work_blocks = arrived.reshape(col_count * capacity, block_size, block_size)
    flat_places = arrived_places.reshape(col_count * capacity, 2)
    work_rows = flat_places[:, 0]
    work_cols = flat_places[:, 1]

    def backward(left_bf):
        return backward_terms(left_bf, work_blocks, work_rows, work_cols, TC)

    def sum_right(partial_value):
        return big_sum(partial_value, "row")

    def finish_left(unscaled, need_form):
        squares = jnp.sum(unscaled * unscaled, axis=1)
        total = small_sum(squares, "row")
        beta_norm = jnp.sqrt(total + EPSILON)
        scaled = unscaled / beta_norm[:, None]
        rounded = None
        if need_form:
            rounded = scaled.astype(jnp.bfloat16)
        return (beta_norm, scaled, rounded)

    def finish_right(unscaled):
        squares = jnp.sum(unscaled * unscaled, axis=1)
        total = small_sum(squares, "col")
        alpha_norm = jnp.sqrt(total + EPSILON)
        scaled = unscaled / alpha_norm[:, None]
        rounded = scaled.astype(jnp.bfloat16)
        return (alpha_norm, scaled, rounded)

    beta_norm, left_vec, left_bf = finish_left(right_side, True)
    alpha_norm, right_vec, right_bf = finish_right(sum_right(backward(left_bf)))
    search = right_vec
    solution = jnp.zeros_like(right_vec)
    phibar = beta_norm
    rhobar = alpha_norm
    for iteration in range(ITERS):
        last_turn = iteration + 1 == ITERS
        unscaled = (
            big_sum(forward_terms(right_bf, work_blocks, work_rows, work_cols, row_tiles), "col")
            - alpha_norm[:, None] * left_vec
        )
        beta_norm, left_vec, left_bf = finish_left(unscaled, not last_turn)
        rho_value = jnp.sqrt(rhobar * rhobar + beta_norm * beta_norm)
        cosine = rhobar / rho_value
        sine_value = beta_norm / rho_value
        phi_value = cosine * phibar
        phibar = sine_value * phibar
        solution = solution + (phi_value / rho_value)[:, None] * search
        if not last_turn:
            unscaled = sum_right(backward(left_bf)) - beta_norm[:, None] * right_vec
            alpha_norm, right_vec, right_bf = finish_right(unscaled)
            theta_value = sine_value * alpha_norm
            rhobar = -cosine * alpha_norm
            search = right_vec - (theta_value / rho_value)[:, None] * search
    share_len = solution.shape[1] // row_count
    solution = lax.dynamic_slice_in_dim(solution, lax.axis_index("row") * share_len, share_len, 1)
    return (solution.reshape(snapshots, 1, solution.shape[1]), phibar)


def solution(mesh):
    placed = (
        P(None, "row"),
        P(("row", "col"), None, None),
        P(("row", "col"), None),
        P(("row", "col")),
        P(("row", "col")),
    )
    return jax.shard_map(
        per_device,
        mesh=mesh,
        in_specs=placed,
        out_specs=(P(None, "col", "row"), P()),
        check_vma=False,
    )
```

```python
import jax
import jax.numpy as jnp
from jax import lax
from jax.sharding import PartitionSpec as P

TC = 32
ITERS = 4
CHUNKS = 2


EPSILON = 1e-06


def partner_pairs(count, distance):
    return [(i, i ^ distance) for i in range(count)]


def is_power_of_two(count):
    return count & (count - 1) == 0


def small_sum(value, axis):
    count = lax.axis_size(axis)
    if not is_power_of_two(count):
        return lax.psum(value, axis)
    distance = 1
    while distance < count:
        value = value + lax.ppermute(value, axis, partner_pairs(count, distance))
        distance *= 2
    return value


def big_sum(value, axis):
    count = lax.axis_size(axis)
    width = value.shape[-1]
    if not is_power_of_two(count) or width % (128 * count):
        return lax.psum(value, axis)
    index = lax.axis_index(axis)
    distances = []
    distance = 1
    while distance < count:
        distances.append(distance)
        distance *= 2
    lanes = jnp.split(value, CHUNKS, axis=0)
    last = distances.pop()
    if len(distances) > 1:
        distances[0], distances[1] = distances[1], distances[0]
    for distance in distances:
        upper = (index // distance) % 2
        moved = []
        for held in lanes:
            half = held.shape[-1] // 2
            keep = lax.dynamic_slice_in_dim(held, upper * half, half, held.ndim - 1)
            give = lax.dynamic_slice_in_dim(held, (1 - upper) * half, half, held.ndim - 1)
            moved.append(keep + lax.ppermute(give, axis, partner_pairs(count, distance)))
        lanes = moved
    lanes = [held + lax.ppermute(held, axis, partner_pairs(count, last)) for held in lanes]
    for distance in reversed(distances):
        upper = (index // distance) % 2
        moved = []
        for held in lanes:
            other = lax.ppermute(held, axis, partner_pairs(count, distance))
            moved.append(jnp.where(
                upper == 1,
                jnp.concatenate([other, held], axis=-1),
                jnp.concatenate([held, other], axis=-1),
            ))
        lanes = moved
    return jnp.concatenate(lanes, axis=0)


def gather_tiles(vector_bf, indices, block_size):
    snapshots, extent = vector_bf.shape
    vector_tiles = vector_bf.reshape(snapshots, extent // block_size, block_size)
    return jnp.take(vector_tiles, indices, axis=1)


def place_terms(weighted, indices, n_out):
    snapshots, number, block_size = weighted.shape
    onehot = (indices[:, None] == jnp.arange(n_out, dtype=jnp.int32)[None, :]).astype(jnp.float32)
    summed = jnp.einsum("ksi,st->kti", weighted, onehot, precision=lax.Precision.HIGH)
    return summed.reshape(snapshots, n_out * block_size)


def forward_terms(vector_bf, blocks, row_index, col_index, n_out):
    picked = gather_tiles(vector_bf, col_index, blocks.shape[1])
    weighted = jnp.einsum("sij,ksj->ksi", blocks, picked, preferred_element_type=jnp.float32)
    return place_terms(weighted, row_index, n_out)


def backward_terms(vector_bf, blocks, row_index, col_index, n_out):
    picked = gather_tiles(vector_bf, row_index, blocks.shape[1])
    weighted = jnp.einsum("sji,ksj->ksi", blocks, picked, preferred_element_type=jnp.float32)
    return place_terms(weighted, col_index, n_out)


def per_device(right_side, blocks, targets, tile_rows, tile_cols):
    col_count = lax.axis_size("col")
    row_count = lax.axis_size("row")
    block_size = blocks.shape[1]
    snapshots = right_side.shape[0]
    row_tiles = right_side.shape[1] // block_size
    own_count = blocks.shape[0]
    capacity = 2 * own_count // col_count
    target = targets[:, 0]
    slot_count = col_count * capacity
    matches = (target[:, None] == jnp.arange(col_count, dtype=jnp.int32)[None, :]).astype(jnp.int32)
    before = jnp.cumsum(matches, axis=0) - matches
    slot_index = target * capacity + jnp.sum(before * matches, axis=1)
    pick = slot_index[:, None] == jnp.arange(slot_count, dtype=jnp.int32)[None, :]
    source = jnp.sum(jnp.where(pick, jnp.arange(own_count, dtype=jnp.int32)[:, None], 0), axis=0)
    source = jnp.where(jnp.any(pick, axis=0), source, own_count)
    padded = jnp.concatenate([blocks, jnp.zeros((1, block_size, block_size), blocks.dtype)], axis=0)
    outgoing = jnp.take(padded, source, axis=0, mode="clip")
    padded_places = jnp.concatenate(
        [jnp.stack([tile_rows, tile_cols], axis=1), jnp.zeros((1, 2), jnp.int32)], axis=0
    )
    places = jnp.take(padded_places, source, axis=0, mode="clip")
    arrived, arrived_places = (
        lax.all_to_all(
            outgoing.reshape(col_count, capacity, block_size, block_size),
            "col",
            split_axis=0,
            concat_axis=0,
            tiled=True,
        ),
        lax.all_to_all(
            places.reshape(col_count, capacity, 2), "col", split_axis=0, concat_axis=0, tiled=True
        ),
    )
    work_blocks = arrived.reshape(col_count * capacity, block_size, block_size)
    flat_places = arrived_places.reshape(col_count * capacity, 2)
    work_rows = flat_places[:, 0]
    work_cols = flat_places[:, 1]

    def backward(left_bf):
        return backward_terms(left_bf, work_blocks, work_rows, work_cols, TC)

    def sum_right(partial_value):
        return big_sum(partial_value, "row")

    def finish_left(unscaled, need_form):
        squares = jnp.sum(unscaled * unscaled, axis=1)
        total = small_sum(squares, "row")
        beta_norm = jnp.sqrt(total + EPSILON)
        scaled = unscaled / beta_norm[:, None]
        rounded = None
        if need_form:
            rounded = scaled.astype(jnp.bfloat16)
        return (beta_norm, scaled, rounded)

    def finish_right(unscaled):
        squares = jnp.sum(unscaled * unscaled, axis=1)
        total = small_sum(squares, "col")
        alpha_norm = jnp.sqrt(total + EPSILON)
        scaled = unscaled / alpha_norm[:, None]
        rounded = scaled.astype(jnp.bfloat16)
        return (alpha_norm, scaled, rounded)

    beta_norm, left_vec, left_bf = finish_left(right_side, True)
    alpha_norm, right_vec, right_bf = finish_right(sum_right(backward(left_bf)))
    search = right_vec
    solution = jnp.zeros_like(right_vec)
    phibar = beta_norm
    rhobar = alpha_norm
    for iteration in range(ITERS):
        last_turn = iteration + 1 == ITERS
        unscaled = (
            big_sum(forward_terms(right_bf, work_blocks, work_rows, work_cols, row_tiles), "col")
            - alpha_norm[:, None] * left_vec
        )
        beta_norm, left_vec, left_bf = finish_left(unscaled, not last_turn)
        rho_value = jnp.sqrt(rhobar * rhobar + beta_norm * beta_norm)
        cosine = rhobar / rho_value
        sine_value = beta_norm / rho_value
        phi_value = cosine * phibar
        phibar = sine_value * phibar
        solution = solution + (phi_value / rho_value)[:, None] * search
        if not last_turn:
            unscaled = sum_right(backward(left_bf)) - beta_norm[:, None] * right_vec
            alpha_norm, right_vec, right_bf = finish_right(unscaled)
            theta_value = sine_value * alpha_norm
            rhobar = -cosine * alpha_norm
            search = right_vec - (theta_value / rho_value)[:, None] * search
    share_len = solution.shape[1] // row_count
    solution = lax.dynamic_slice_in_dim(solution, lax.axis_index("row") * share_len, share_len, 1)
    return (solution.reshape(snapshots, 1, solution.shape[1]), phibar)


def solution(mesh):
    placed = (
        P(None, "row"),
        P(("row", "col"), None, None),
        P(("row", "col"), None),
        P(("row", "col")),
        P(("row", "col")),
    )
    return jax.shard_map(
        per_device,
        mesh=mesh,
        in_specs=placed,
        out_specs=(P(None, "col", "row"), P()),
        check_vma=False,
    )
```

```python
import jax
import jax.numpy as jnp
from jax import lax
from jax.sharding import PartitionSpec as P

TC = 32
ITERS = 4
CHUNKS = 2


EPSILON = 1e-06


def partner_pairs(count, distance):
    return [(i, i ^ distance) for i in range(count)]


def is_power_of_two(count):
    return count & (count - 1) == 0


def small_sum(value, axis):
    count = lax.axis_size(axis)
    if not is_power_of_two(count):
        return lax.psum(value, axis)
    distance = 1
    while distance < count:
        value = value + lax.ppermute(value, axis, partner_pairs(count, distance))
        distance *= 2
    return value


def big_sum(value, axis):
    count = lax.axis_size(axis)
    width = value.shape[-1]
    if not is_power_of_two(count) or width % (128 * count):
        return lax.psum(value, axis)
    index = lax.axis_index(axis)
    distances = []
    distance = 1
    while distance < count:
        distances.append(distance)
        distance *= 2
    lanes = jnp.split(value, CHUNKS, axis=0)
    last = distances.pop()
    orders = [distances[lane % len(distances):] + distances[:lane % len(distances)] if distances else [] for lane in range(CHUNKS)]
    for step in range(len(distances)):
        moved = []
        for lane, held in enumerate(lanes):
            distance = orders[lane][step]
            upper = (index // distance) % 2
            half = held.shape[-1] // 2
            keep = lax.dynamic_slice_in_dim(held, upper * half, half, held.ndim - 1)
            give = lax.dynamic_slice_in_dim(held, (1 - upper) * half, half, held.ndim - 1)
            moved.append(keep + lax.ppermute(give, axis, partner_pairs(count, distance)))
        lanes = moved
    lanes = [held + lax.ppermute(held, axis, partner_pairs(count, last)) for held in lanes]
    for step in reversed(range(len(distances))):
        moved = []
        for lane, held in enumerate(lanes):
            distance = orders[lane][step]
            upper = (index // distance) % 2
            other = lax.ppermute(held, axis, partner_pairs(count, distance))
            moved.append(jnp.where(
                upper == 1,
                jnp.concatenate([other, held], axis=-1),
                jnp.concatenate([held, other], axis=-1),
            ))
        lanes = moved
    return jnp.concatenate(lanes, axis=0)


def gather_tiles(vector_bf, indices, block_size):
    snapshots, extent = vector_bf.shape
    vector_tiles = vector_bf.reshape(snapshots, extent // block_size, block_size)
    return jnp.take(vector_tiles, indices, axis=1)


def place_terms(weighted, indices, n_out):
    snapshots, number, block_size = weighted.shape
    onehot = (indices[:, None] == jnp.arange(n_out, dtype=jnp.int32)[None, :]).astype(jnp.float32)
    summed = jnp.einsum("ksi,st->kti", weighted, onehot, precision=lax.Precision.HIGH)
    return summed.reshape(snapshots, n_out * block_size)


def forward_terms(vector_bf, blocks, row_index, col_index, n_out):
    picked = gather_tiles(vector_bf, col_index, blocks.shape[1])
    weighted = jnp.einsum("sij,ksj->ksi", blocks, picked, preferred_element_type=jnp.float32)
    return place_terms(weighted, row_index, n_out)


def backward_terms(vector_bf, blocks, row_index, col_index, n_out):
    picked = gather_tiles(vector_bf, row_index, blocks.shape[1])
    weighted = jnp.einsum("sji,ksj->ksi", blocks, picked, preferred_element_type=jnp.float32)
    return place_terms(weighted, col_index, n_out)


def per_device(right_side, blocks, targets, tile_rows, tile_cols):
    col_count = lax.axis_size("col")
    row_count = lax.axis_size("row")
    block_size = blocks.shape[1]
    snapshots = right_side.shape[0]
    row_tiles = right_side.shape[1] // block_size
    own_count = blocks.shape[0]
    capacity = 2 * own_count // col_count
    target = targets[:, 0]
    slot_count = col_count * capacity
    matches = (target[:, None] == jnp.arange(col_count, dtype=jnp.int32)[None, :]).astype(jnp.int32)
    before = jnp.cumsum(matches, axis=0) - matches
    slot_index = target * capacity + jnp.sum(before * matches, axis=1)
    pick = slot_index[:, None] == jnp.arange(slot_count, dtype=jnp.int32)[None, :]
    source = jnp.sum(jnp.where(pick, jnp.arange(own_count, dtype=jnp.int32)[:, None], 0), axis=0)
    source = jnp.where(jnp.any(pick, axis=0), source, own_count)
    padded = jnp.concatenate([blocks, jnp.zeros((1, block_size, block_size), blocks.dtype)], axis=0)
    outgoing = jnp.take(padded, source, axis=0, mode="clip")
    padded_places = jnp.concatenate(
        [jnp.stack([tile_rows, tile_cols], axis=1), jnp.zeros((1, 2), jnp.int32)], axis=0
    )
    places = jnp.take(padded_places, source, axis=0, mode="clip")
    arrived, arrived_places = (
        lax.all_to_all(
            outgoing.reshape(col_count, capacity, block_size, block_size),
            "col",
            split_axis=0,
            concat_axis=0,
            tiled=True,
        ),
        lax.all_to_all(
            places.reshape(col_count, capacity, 2), "col", split_axis=0, concat_axis=0, tiled=True
        ),
    )
    work_blocks = arrived.reshape(col_count * capacity, block_size, block_size)
    flat_places = arrived_places.reshape(col_count * capacity, 2)
    work_rows = flat_places[:, 0]
    work_cols = flat_places[:, 1]

    def backward(left_bf):
        return backward_terms(left_bf, work_blocks, work_rows, work_cols, TC)

    def sum_right(partial_value):
        return big_sum(partial_value, "row")

    def finish_left(unscaled, need_form):
        squares = jnp.sum(unscaled * unscaled, axis=1)
        total = small_sum(squares, "row")
        beta_norm = jnp.sqrt(total + EPSILON)
        scaled = unscaled / beta_norm[:, None]
        rounded = None
        if need_form:
            rounded = scaled.astype(jnp.bfloat16)
        return (beta_norm, scaled, rounded)

    def finish_right(unscaled):
        squares = jnp.sum(unscaled * unscaled, axis=1)
        total = small_sum(squares, "col")
        alpha_norm = jnp.sqrt(total + EPSILON)
        scaled = unscaled / alpha_norm[:, None]
        rounded = scaled.astype(jnp.bfloat16)
        return (alpha_norm, scaled, rounded)

    beta_norm, left_vec, left_bf = finish_left(right_side, True)
    alpha_norm, right_vec, right_bf = finish_right(sum_right(backward(left_bf)))
    search = right_vec
    solution = jnp.zeros_like(right_vec)
    phibar = beta_norm
    rhobar = alpha_norm
    for iteration in range(ITERS):
        last_turn = iteration + 1 == ITERS
        unscaled = (
            big_sum(forward_terms(right_bf, work_blocks, work_rows, work_cols, row_tiles), "col")
            - alpha_norm[:, None] * left_vec
        )
        beta_norm, left_vec, left_bf = finish_left(unscaled, not last_turn)
        rho_value = jnp.sqrt(rhobar * rhobar + beta_norm * beta_norm)
        cosine = rhobar / rho_value
        sine_value = beta_norm / rho_value
        phi_value = cosine * phibar
        phibar = sine_value * phibar
        solution = solution + (phi_value / rho_value)[:, None] * search
        if not last_turn:
            unscaled = sum_right(backward(left_bf)) - beta_norm[:, None] * right_vec
            alpha_norm, right_vec, right_bf = finish_right(unscaled)
            theta_value = sine_value * alpha_norm
            rhobar = -cosine * alpha_norm
            search = right_vec - (theta_value / rho_value)[:, None] * search
    share_len = solution.shape[1] // row_count
    solution = lax.dynamic_slice_in_dim(solution, lax.axis_index("row") * share_len, share_len, 1)
    return (solution.reshape(snapshots, 1, solution.shape[1]), phibar)


def solution(mesh):
    placed = (
        P(None, "row"),
        P(("row", "col"), None, None),
        P(("row", "col"), None),
        P(("row", "col")),
        P(("row", "col")),
    )
    return jax.shard_map(
        per_device,
        mesh=mesh,
        in_specs=placed,
        out_specs=(P(None, "col", "row"), P()),
        check_vma=False,
    )
```

```python
import jax
import jax.numpy as jnp
from jax import lax
from jax.sharding import PartitionSpec as P

TC = 32
ITERS = 4
CHUNKS = 2


EPSILON = 1e-06


def partner_pairs(count, distance):
    return [(i, i ^ distance) for i in range(count)]


def is_power_of_two(count):
    return count & (count - 1) == 0


def small_sum(value, axis):
    count = lax.axis_size(axis)
    if not is_power_of_two(count):
        return lax.psum(value, axis)
    distance = 1
    while distance < count:
        value = value + lax.ppermute(value, axis, partner_pairs(count, distance))
        distance *= 2
    return value


def big_sum(value, axis):
    count = lax.axis_size(axis)
    width = value.shape[-1]
    if not is_power_of_two(count) or width % (128 * count):
        return lax.psum(value, axis)
    index = lax.axis_index(axis)
    distances = []
    distance = 1
    while distance < count:
        distances.append(distance)
        distance *= 2
    lanes = jnp.split(value, CHUNKS, axis=0)
    last = distances.pop()
    orders = [distances[lane % len(distances):] + distances[:lane % len(distances)] if distances else [] for lane in range(CHUNKS)]
    for step in range(len(distances)):
        moved = []
        for lane, held in enumerate(lanes):
            distance = orders[lane][step]
            upper = (index // distance) % 2
            half = held.shape[-1] // 2
            keep = lax.dynamic_slice_in_dim(held, upper * half, half, held.ndim - 1)
            give = lax.dynamic_slice_in_dim(held, (1 - upper) * half, half, held.ndim - 1)
            moved.append(keep + lax.ppermute(give, axis, partner_pairs(count, distance)))
        lanes = moved
    lanes = [held + lax.ppermute(held, axis, partner_pairs(count, last)) for held in lanes]
    for step in reversed(range(len(distances))):
        moved = []
        for lane, held in enumerate(lanes):
            distance = orders[lane][step]
            upper = (index // distance) % 2
            other = lax.ppermute(held, axis, partner_pairs(count, distance))
            moved.append(jnp.where(
                upper == 1,
                jnp.concatenate([other, held], axis=-1),
                jnp.concatenate([held, other], axis=-1),
            ))
        lanes = moved
    return jnp.concatenate(lanes, axis=0)


def gather_tiles(vector_bf, indices, block_size):
    snapshots, extent = vector_bf.shape
    vector_tiles = vector_bf.reshape(snapshots, extent // block_size, block_size)
    onehot = (indices[:, None] == jnp.arange(extent // block_size, dtype=jnp.int32)[None, :]).astype(vector_bf.dtype)
    picked = jnp.einsum("ktj,st->ksj", vector_tiles, onehot, preferred_element_type=jnp.float32)
    return picked.astype(vector_bf.dtype)


def place_terms(weighted, indices, n_out):
    snapshots, number, block_size = weighted.shape
    onehot = (indices[:, None] == jnp.arange(n_out, dtype=jnp.int32)[None, :]).astype(jnp.float32)
    summed = jnp.einsum("ksi,st->kti", weighted, onehot, precision=lax.Precision.HIGH)
    return summed.reshape(snapshots, n_out * block_size)


def forward_terms(vector_bf, blocks, row_index, col_index, n_out):
    picked = gather_tiles(vector_bf, col_index, blocks.shape[1])
    weighted = jnp.einsum("sij,ksj->ksi", blocks, picked, preferred_element_type=jnp.float32)
    return place_terms(weighted, row_index, n_out)


def backward_terms(vector_bf, blocks, row_index, col_index, n_out):
    picked = gather_tiles(vector_bf, row_index, blocks.shape[1])
    weighted = jnp.einsum("sji,ksj->ksi", blocks, picked, preferred_element_type=jnp.float32)
    return place_terms(weighted, col_index, n_out)


def per_device(right_side, blocks, targets, tile_rows, tile_cols):
    col_count = lax.axis_size("col")
    row_count = lax.axis_size("row")
    block_size = blocks.shape[1]
    snapshots = right_side.shape[0]
    row_tiles = right_side.shape[1] // block_size
    own_count = blocks.shape[0]
    capacity = 2 * own_count // col_count
    target = targets[:, 0]
    slot_count = col_count * capacity
    matches = (target[:, None] == jnp.arange(col_count, dtype=jnp.int32)[None, :]).astype(jnp.int32)
    before = jnp.cumsum(matches, axis=0) - matches
    slot_index = target * capacity + jnp.sum(before * matches, axis=1)
    pick = slot_index[:, None] == jnp.arange(slot_count, dtype=jnp.int32)[None, :]
    source = jnp.sum(jnp.where(pick, jnp.arange(own_count, dtype=jnp.int32)[:, None], 0), axis=0)
    source = jnp.where(jnp.any(pick, axis=0), source, own_count)
    padded = jnp.concatenate([blocks, jnp.zeros((1, block_size, block_size), blocks.dtype)], axis=0)
    outgoing = jnp.take(padded, source, axis=0, mode="clip")
    padded_places = jnp.concatenate(
        [jnp.stack([tile_rows, tile_cols], axis=1), jnp.zeros((1, 2), jnp.int32)], axis=0
    )
    places = jnp.take(padded_places, source, axis=0, mode="clip")
    arrived, arrived_places = (
        lax.all_to_all(
            outgoing.reshape(col_count, capacity, block_size, block_size),
            "col",
            split_axis=0,
            concat_axis=0,
            tiled=True,
        ),
        lax.all_to_all(
            places.reshape(col_count, capacity, 2), "col", split_axis=0, concat_axis=0, tiled=True
        ),
    )
    work_blocks = arrived.reshape(col_count * capacity, block_size, block_size)
    flat_places = arrived_places.reshape(col_count * capacity, 2)
    work_rows = flat_places[:, 0]
    work_cols = flat_places[:, 1]

    def backward(left_bf):
        return backward_terms(left_bf, work_blocks, work_rows, work_cols, TC)

    def sum_right(partial_value):
        return big_sum(partial_value, "row")

    def finish_left(unscaled, need_form):
        squares = jnp.sum(unscaled * unscaled, axis=1)
        total = small_sum(squares, "row")
        beta_norm = jnp.sqrt(total + EPSILON)
        scaled = unscaled / beta_norm[:, None]
        rounded = None
        if need_form:
            rounded = scaled.astype(jnp.bfloat16)
        return (beta_norm, scaled, rounded)

    def finish_right(unscaled):
        squares = jnp.sum(unscaled * unscaled, axis=1)
        total = small_sum(squares, "col")
        alpha_norm = jnp.sqrt(total + EPSILON)
        scaled = unscaled / alpha_norm[:, None]
        rounded = scaled.astype(jnp.bfloat16)
        return (alpha_norm, scaled, rounded)

    beta_norm, left_vec, left_bf = finish_left(right_side, True)
    alpha_norm, right_vec, right_bf = finish_right(sum_right(backward(left_bf)))
    search = right_vec
    solution = jnp.zeros_like(right_vec)
    phibar = beta_norm
    rhobar = alpha_norm
    for iteration in range(ITERS):
        last_turn = iteration + 1 == ITERS
        unscaled = (
            big_sum(forward_terms(right_bf, work_blocks, work_rows, work_cols, row_tiles), "col")
            - alpha_norm[:, None] * left_vec
        )
        beta_norm, left_vec, left_bf = finish_left(unscaled, not last_turn)
        rho_value = jnp.sqrt(rhobar * rhobar + beta_norm * beta_norm)
        cosine = rhobar / rho_value
        sine_value = beta_norm / rho_value
        phi_value = cosine * phibar
        phibar = sine_value * phibar
        solution = solution + (phi_value / rho_value)[:, None] * search
        if not last_turn:
            unscaled = sum_right(backward(left_bf)) - beta_norm[:, None] * right_vec
            alpha_norm, right_vec, right_bf = finish_right(unscaled)
            theta_value = sine_value * alpha_norm
            rhobar = -cosine * alpha_norm
            search = right_vec - (theta_value / rho_value)[:, None] * search
    share_len = solution.shape[1] // row_count
    solution = lax.dynamic_slice_in_dim(solution, lax.axis_index("row") * share_len, share_len, 1)
    return (solution.reshape(snapshots, 1, solution.shape[1]), phibar)


def solution(mesh):
    placed = (
        P(None, "row"),
        P(("row", "col"), None, None),
        P(("row", "col"), None),
        P(("row", "col")),
        P(("row", "col")),
    )
    return jax.shard_map(
        per_device,
        mesh=mesh,
        in_specs=placed,
        out_specs=(P(None, "col", "row"), P()),
        check_vma=False,
    )
```

```python
import jax
import jax.numpy as jnp
from jax import lax
from jax.sharding import PartitionSpec as P

TC = 32
ITERS = 4
CHUNKS = 2


EPSILON = 1e-06


def partner_pairs(count, distance):
    return [(i, i ^ distance) for i in range(count)]


def is_power_of_two(count):
    return count & (count - 1) == 0


def gathered_sum(value, axis):
    count = lax.axis_size(axis)
    me = lax.axis_index(axis)
    arrived = [value] + [
        lax.ppermute(value, axis, [(i, (i + shift) % count) for i in range(count)])
        for shift in range(1, count)
    ]
    stacked = jnp.stack(arrived, axis=0)
    ordered = jnp.take(stacked, (me - jnp.arange(count)) % count, axis=0)
    total = ordered[0]
    for source in range(1, count):
        total = total + ordered[source]
    return total


def small_sum(value, axis):
    count = lax.axis_size(axis)
    if axis == "col":
        return gathered_sum(value, axis)
    if not is_power_of_two(count):
        return lax.psum(value, axis)
    distance = 1
    while distance < count:
        value = value + lax.ppermute(value, axis, partner_pairs(count, distance))
        distance *= 2
    return value


def big_sum(value, axis):
    count = lax.axis_size(axis)
    width = value.shape[-1]
    if not is_power_of_two(count) or width % (128 * count):
        return lax.psum(value, axis)
    index = lax.axis_index(axis)
    distances = []
    distance = 1
    while distance < count:
        distances.append(distance)
        distance *= 2
    lanes = jnp.split(value, CHUNKS, axis=0)
    last = distances.pop()
    orders = [distances[lane % len(distances):] + distances[:lane % len(distances)] if distances else [] for lane in range(CHUNKS)]
    for step in range(len(distances)):
        moved = []
        for lane, held in enumerate(lanes):
            distance = orders[lane][step]
            upper = (index // distance) % 2
            half = held.shape[-1] // 2
            keep = lax.dynamic_slice_in_dim(held, upper * half, half, held.ndim - 1)
            give = lax.dynamic_slice_in_dim(held, (1 - upper) * half, half, held.ndim - 1)
            moved.append(keep + lax.ppermute(give, axis, partner_pairs(count, distance)))
        lanes = moved
    lanes = [held + lax.ppermute(held, axis, partner_pairs(count, last)) for held in lanes]
    for step in reversed(range(len(distances))):
        moved = []
        for lane, held in enumerate(lanes):
            distance = orders[lane][step]
            upper = (index // distance) % 2
            other = lax.ppermute(held, axis, partner_pairs(count, distance))
            moved.append(jnp.where(
                upper == 1,
                jnp.concatenate([other, held], axis=-1),
                jnp.concatenate([held, other], axis=-1),
            ))
        lanes = moved
    return jnp.concatenate(lanes, axis=0)


def gather_tiles(vector_bf, indices, block_size):
    snapshots, extent = vector_bf.shape
    vector_tiles = vector_bf.reshape(snapshots, extent // block_size, block_size)
    return jnp.take(vector_tiles, indices, axis=1)


def place_terms(weighted, indices, n_out):
    snapshots, number, block_size = weighted.shape
    onehot = (indices[:, None] == jnp.arange(n_out, dtype=jnp.int32)[None, :]).astype(jnp.float32)
    summed = jnp.einsum("ksi,st->kti", weighted, onehot, precision=lax.Precision.HIGH)
    return summed.reshape(snapshots, n_out * block_size)


def forward_terms(vector_bf, blocks, row_index, col_index, n_out):
    picked = gather_tiles(vector_bf, col_index, blocks.shape[1])
    weighted = jnp.einsum("sij,ksj->ksi", blocks, picked, preferred_element_type=jnp.float32)
    return place_terms(weighted, row_index, n_out)


def backward_terms(vector_bf, blocks, row_index, col_index, n_out):
    picked = gather_tiles(vector_bf, row_index, blocks.shape[1])
    weighted = jnp.einsum("sji,ksj->ksi", blocks, picked, preferred_element_type=jnp.float32)
    return place_terms(weighted, col_index, n_out)


def per_device(right_side, blocks, targets, tile_rows, tile_cols):
    col_count = lax.axis_size("col")
    row_count = lax.axis_size("row")
    block_size = blocks.shape[1]
    snapshots = right_side.shape[0]
    row_tiles = right_side.shape[1] // block_size
    own_count = blocks.shape[0]
    capacity = 2 * own_count // col_count
    target = targets[:, 0]
    slot_count = col_count * capacity
    matches = (target[:, None] == jnp.arange(col_count, dtype=jnp.int32)[None, :]).astype(jnp.int32)
    before = jnp.cumsum(matches, axis=0) - matches
    slot_index = target * capacity + jnp.sum(before * matches, axis=1)
    pick = slot_index[:, None] == jnp.arange(slot_count, dtype=jnp.int32)[None, :]
    source = jnp.sum(jnp.where(pick, jnp.arange(own_count, dtype=jnp.int32)[:, None], 0), axis=0)
    source = jnp.where(jnp.any(pick, axis=0), source, own_count)
    padded = jnp.concatenate([blocks, jnp.zeros((1, block_size, block_size), blocks.dtype)], axis=0)
    outgoing = jnp.take(padded, source, axis=0, mode="clip")
    padded_places = jnp.concatenate(
        [jnp.stack([tile_rows, tile_cols], axis=1), jnp.zeros((1, 2), jnp.int32)], axis=0
    )
    places = jnp.take(padded_places, source, axis=0, mode="clip")
    arrived, arrived_places = (
        lax.all_to_all(
            outgoing.reshape(col_count, capacity, block_size, block_size),
            "col",
            split_axis=0,
            concat_axis=0,
            tiled=True,
        ),
        lax.all_to_all(
            places.reshape(col_count, capacity, 2), "col", split_axis=0, concat_axis=0, tiled=True
        ),
    )
    work_blocks = arrived.reshape(col_count * capacity, block_size, block_size)
    flat_places = arrived_places.reshape(col_count * capacity, 2)
    work_rows = flat_places[:, 0]
    work_cols = flat_places[:, 1]

    def backward(left_bf):
        return backward_terms(left_bf, work_blocks, work_rows, work_cols, TC)

    def sum_right(partial_value):
        return big_sum(partial_value, "row")

    def finish_left(unscaled, need_form):
        squares = jnp.sum(unscaled * unscaled, axis=1)
        total = small_sum(squares, "row")
        beta_norm = jnp.sqrt(total + EPSILON)
        scaled = unscaled / beta_norm[:, None]
        rounded = None
        if need_form:
            rounded = scaled.astype(jnp.bfloat16)
        return (beta_norm, scaled, rounded)

    def finish_right(unscaled):
        squares = jnp.sum(unscaled * unscaled, axis=1)
        total = small_sum(squares, "col")
        alpha_norm = jnp.sqrt(total + EPSILON)
        scaled = unscaled / alpha_norm[:, None]
        rounded = scaled.astype(jnp.bfloat16)
        return (alpha_norm, scaled, rounded)

    beta_norm, left_vec, left_bf = finish_left(right_side, True)
    alpha_norm, right_vec, right_bf = finish_right(sum_right(backward(left_bf)))
    search = right_vec
    solution = jnp.zeros_like(right_vec)
    phibar = beta_norm
    rhobar = alpha_norm
    for iteration in range(ITERS):
        last_turn = iteration + 1 == ITERS
        unscaled = (
            big_sum(forward_terms(right_bf, work_blocks, work_rows, work_cols, row_tiles), "col")
            - alpha_norm[:, None] * left_vec
        )
        beta_norm, left_vec, left_bf = finish_left(unscaled, not last_turn)
        rho_value = jnp.sqrt(rhobar * rhobar + beta_norm * beta_norm)
        cosine = rhobar / rho_value
        sine_value = beta_norm / rho_value
        phi_value = cosine * phibar
        phibar = sine_value * phibar
        solution = solution + (phi_value / rho_value)[:, None] * search
        if not last_turn:
            unscaled = sum_right(backward(left_bf)) - beta_norm[:, None] * right_vec
            alpha_norm, right_vec, right_bf = finish_right(unscaled)
            theta_value = sine_value * alpha_norm
            rhobar = -cosine * alpha_norm
            search = right_vec - (theta_value / rho_value)[:, None] * search
    share_len = solution.shape[1] // row_count
    solution = lax.dynamic_slice_in_dim(solution, lax.axis_index("row") * share_len, share_len, 1)
    return (solution.reshape(snapshots, 1, solution.shape[1]), phibar)


def solution(mesh):
    placed = (
        P(None, "row"),
        P(("row", "col"), None, None),
        P(("row", "col"), None),
        P(("row", "col")),
        P(("row", "col")),
    )
    return jax.shard_map(
        per_device,
        mesh=mesh,
        in_specs=placed,
        out_specs=(P(None, "col", "row"), P()),
        check_vma=False,
    )
```

```python
import jax
import jax.numpy as jnp
from jax import lax
from jax.sharding import PartitionSpec as P

TC = 32
ITERS = 4
CHUNKS = 2


EPSILON = 1e-06


def partner_pairs(count, distance):
    return [(i, i ^ distance) for i in range(count)]


def is_power_of_two(count):
    return count & (count - 1) == 0


def small_sum(value, axis):
    count = lax.axis_size(axis)
    if not is_power_of_two(count):
        return lax.psum(value, axis)
    distance = 1
    while distance < count:
        value = value + lax.ppermute(value, axis, partner_pairs(count, distance))
        distance *= 2
    return value


def big_sum(value, axis):
    count = lax.axis_size(axis)
    width = value.shape[-1]
    if not is_power_of_two(count) or width % (128 * count):
        return lax.psum(value, axis)
    index = lax.axis_index(axis)
    distances = []
    distance = 1
    while distance < count:
        distances.append(distance)
        distance *= 2
    lanes = jnp.split(value, CHUNKS, axis=0)
    orders = [distances[lane % len(distances):] + distances[:lane % len(distances)] for lane in range(CHUNKS)]
    lasts = [order.pop() for order in orders]
    for step in range(len(distances) - 1):
        moved = []
        for lane, held in enumerate(lanes):
            distance = orders[lane][step]
            upper = (index // distance) % 2
            half = held.shape[-1] // 2
            keep = lax.dynamic_slice_in_dim(held, upper * half, half, held.ndim - 1)
            give = lax.dynamic_slice_in_dim(held, (1 - upper) * half, half, held.ndim - 1)
            moved.append(keep + lax.ppermute(give, axis, partner_pairs(count, distance)))
        lanes = moved
    lanes = [held + lax.ppermute(held, axis, partner_pairs(count, last)) for held, last in zip(lanes, lasts)]
    for step in reversed(range(len(distances) - 1)):
        moved = []
        for lane, held in enumerate(lanes):
            distance = orders[lane][step]
            upper = (index // distance) % 2
            other = lax.ppermute(held, axis, partner_pairs(count, distance))
            moved.append(jnp.where(
                upper == 1,
                jnp.concatenate([other, held], axis=-1),
                jnp.concatenate([held, other], axis=-1),
            ))
        lanes = moved
    return jnp.concatenate(lanes, axis=0)


def gather_tiles(vector_bf, indices, block_size):
    snapshots, extent = vector_bf.shape
    vector_tiles = vector_bf.reshape(snapshots, extent // block_size, block_size)
    return jnp.take(vector_tiles, indices, axis=1)


def place_terms(weighted, indices, n_out):
    snapshots, number, block_size = weighted.shape
    onehot = (indices[:, None] == jnp.arange(n_out, dtype=jnp.int32)[None, :]).astype(jnp.float32)
    summed = jnp.einsum("ksi,st->kti", weighted, onehot, precision=lax.Precision.HIGH)
    return summed.reshape(snapshots, n_out * block_size)


def forward_terms(vector_bf, blocks, row_index, col_index, n_out):
    picked = gather_tiles(vector_bf, col_index, blocks.shape[1])
    weighted = jnp.einsum("sij,ksj->ksi", blocks, picked, preferred_element_type=jnp.float32)
    return place_terms(weighted, row_index, n_out)


def backward_terms(vector_bf, blocks, row_index, col_index, n_out):
    picked = gather_tiles(vector_bf, row_index, blocks.shape[1])
    weighted = jnp.einsum("sji,ksj->ksi", blocks, picked, preferred_element_type=jnp.float32)
    return place_terms(weighted, col_index, n_out)


def per_device(right_side, blocks, targets, tile_rows, tile_cols):
    col_count = lax.axis_size("col")
    row_count = lax.axis_size("row")
    block_size = blocks.shape[1]
    snapshots = right_side.shape[0]
    row_tiles = right_side.shape[1] // block_size
    own_count = blocks.shape[0]
    capacity = 2 * own_count // col_count
    target = targets[:, 0]
    slot_count = col_count * capacity
    matches = (target[:, None] == jnp.arange(col_count, dtype=jnp.int32)[None, :]).astype(jnp.int32)
    before = jnp.cumsum(matches, axis=0) - matches
    slot_index = target * capacity + jnp.sum(before * matches, axis=1)
    pick = slot_index[:, None] == jnp.arange(slot_count, dtype=jnp.int32)[None, :]
    source = jnp.sum(jnp.where(pick, jnp.arange(own_count, dtype=jnp.int32)[:, None], 0), axis=0)
    source = jnp.where(jnp.any(pick, axis=0), source, own_count)
    padded = jnp.concatenate([blocks, jnp.zeros((1, block_size, block_size), blocks.dtype)], axis=0)
    outgoing = jnp.take(padded, source, axis=0, mode="clip")
    padded_places = jnp.concatenate(
        [jnp.stack([tile_rows, tile_cols], axis=1), jnp.zeros((1, 2), jnp.int32)], axis=0
    )
    places = jnp.take(padded_places, source, axis=0, mode="clip")
    arrived, arrived_places = (
        lax.all_to_all(
            outgoing.reshape(col_count, capacity, block_size, block_size),
            "col",
            split_axis=0,
            concat_axis=0,
            tiled=True,
        ),
        lax.all_to_all(
            places.reshape(col_count, capacity, 2), "col", split_axis=0, concat_axis=0, tiled=True
        ),
    )
    work_blocks = arrived.reshape(col_count * capacity, block_size, block_size)
    flat_places = arrived_places.reshape(col_count * capacity, 2)
    work_rows = flat_places[:, 0]
    work_cols = flat_places[:, 1]

    def backward(left_bf):
        return backward_terms(left_bf, work_blocks, work_rows, work_cols, TC)

    def sum_right(partial_value):
        return big_sum(partial_value, "row")

    def finish_left(unscaled, need_form):
        squares = jnp.sum(unscaled * unscaled, axis=1)
        total = small_sum(squares, "row")
        beta_norm = jnp.sqrt(total + EPSILON)
        scaled = unscaled / beta_norm[:, None]
        rounded = None
        if need_form:
            rounded = scaled.astype(jnp.bfloat16)
        return (beta_norm, scaled, rounded)

    def finish_right(unscaled):
        squares = jnp.sum(unscaled * unscaled, axis=1)
        total = small_sum(squares, "col")
        alpha_norm = jnp.sqrt(total + EPSILON)
        scaled = unscaled / alpha_norm[:, None]
        rounded = scaled.astype(jnp.bfloat16)
        return (alpha_norm, scaled, rounded)

    beta_norm, left_vec, left_bf = finish_left(right_side, True)
    alpha_norm, right_vec, right_bf = finish_right(sum_right(backward(left_bf)))
    search = right_vec
    solution = jnp.zeros_like(right_vec)
    phibar = beta_norm
    rhobar = alpha_norm
    for iteration in range(ITERS):
        last_turn = iteration + 1 == ITERS
        unscaled = (
            big_sum(forward_terms(right_bf, work_blocks, work_rows, work_cols, row_tiles), "col")
            - alpha_norm[:, None] * left_vec
        )
        beta_norm, left_vec, left_bf = finish_left(unscaled, not last_turn)
        rho_value = jnp.sqrt(rhobar * rhobar + beta_norm * beta_norm)
        cosine = rhobar / rho_value
        sine_value = beta_norm / rho_value
        phi_value = cosine * phibar
        phibar = sine_value * phibar
        solution = solution + (phi_value / rho_value)[:, None] * search
        if not last_turn:
            unscaled = sum_right(backward(left_bf)) - beta_norm[:, None] * right_vec
            alpha_norm, right_vec, right_bf = finish_right(unscaled)
            theta_value = sine_value * alpha_norm
            rhobar = -cosine * alpha_norm
            search = right_vec - (theta_value / rho_value)[:, None] * search
    share_len = solution.shape[1] // row_count
    solution = lax.dynamic_slice_in_dim(solution, lax.axis_index("row") * share_len, share_len, 1)
    return (solution.reshape(snapshots, 1, solution.shape[1]), phibar)


def solution(mesh):
    placed = (
        P(None, "row"),
        P(("row", "col"), None, None),
        P(("row", "col"), None),
        P(("row", "col")),
        P(("row", "col")),
    )
    return jax.shard_map(
        per_device,
        mesh=mesh,
        in_specs=placed,
        out_specs=(P(None, "col", "row"), P()),
        check_vma=False,
    )
```

```python
import jax
import jax.numpy as jnp
from jax import lax
from jax.sharding import PartitionSpec as P

TC = 32
ITERS = 4
CHUNKS = 2


EPSILON = 1e-06


def partner_pairs(count, distance):
    return [(i, i ^ distance) for i in range(count)]


def is_power_of_two(count):
    return count & (count - 1) == 0


def small_sum(value, axis):
    count = lax.axis_size(axis)
    if not is_power_of_two(count):
        return lax.psum(value, axis)
    distance = 1
    while distance < count:
        value = value + lax.ppermute(value, axis, partner_pairs(count, distance))
        distance *= 2
    return value


def big_sum(value, axis):
    count = lax.axis_size(axis)
    width = value.shape[-1]
    if not is_power_of_two(count) or width % (128 * count):
        return lax.psum(value, axis)
    index = lax.axis_index(axis)
    distances = []
    distance = 1
    while distance < count:
        distances.append(distance)
        distance *= 2
    lanes = jnp.split(value, CHUNKS, axis=0)
    if len(distances) == 2:
        orders = [distances[lane % 2:] + distances[:lane % 2] for lane in range(CHUNKS)]
    else:
        orders = [distances[:-1][lane % (len(distances) - 1):] + distances[:-1][:lane % (len(distances) - 1)] + distances[-1:] for lane in range(CHUNKS)]
    lasts = [order.pop() for order in orders]
    distances = distances[:-1]
    for step in range(len(distances)):
        moved = []
        for lane, held in enumerate(lanes):
            distance = orders[lane][step]
            upper = (index // distance) % 2
            half = held.shape[-1] // 2
            keep = lax.dynamic_slice_in_dim(held, upper * half, half, held.ndim - 1)
            give = lax.dynamic_slice_in_dim(held, (1 - upper) * half, half, held.ndim - 1)
            moved.append(keep + lax.ppermute(give, axis, partner_pairs(count, distance)))
        lanes = moved
    lanes = [held + lax.ppermute(held, axis, partner_pairs(count, last)) for held, last in zip(lanes, lasts)]
    for step in reversed(range(len(distances))):
        moved = []
        for lane, held in enumerate(lanes):
            distance = orders[lane][step]
            upper = (index // distance) % 2
            other = lax.ppermute(held, axis, partner_pairs(count, distance))
            moved.append(jnp.where(
                upper == 1,
                jnp.concatenate([other, held], axis=-1),
                jnp.concatenate([held, other], axis=-1),
            ))
        lanes = moved
    return jnp.concatenate(lanes, axis=0)


def gather_tiles(vector_bf, indices, block_size):
    snapshots, extent = vector_bf.shape
    vector_tiles = vector_bf.reshape(snapshots, extent // block_size, block_size)
    return jnp.take(vector_tiles, indices, axis=1)


def place_terms(weighted, indices, n_out):
    snapshots, number, block_size = weighted.shape
    onehot = (indices[:, None] == jnp.arange(n_out, dtype=jnp.int32)[None, :]).astype(jnp.float32)
    summed = jnp.einsum("ksi,st->kti", weighted, onehot, precision=lax.Precision.HIGH)
    return summed.reshape(snapshots, n_out * block_size)


def forward_terms(vector_bf, blocks, row_index, col_index, n_out):
    picked = gather_tiles(vector_bf, col_index, blocks.shape[1])
    weighted = jnp.einsum("sij,ksj->ksi", blocks, picked, preferred_element_type=jnp.float32)
    return place_terms(weighted, row_index, n_out)


def backward_terms(vector_bf, blocks, row_index, col_index, n_out):
    picked = gather_tiles(vector_bf, row_index, blocks.shape[1])
    weighted = jnp.einsum("sji,ksj->ksi", blocks, picked, preferred_element_type=jnp.float32)
    return place_terms(weighted, col_index, n_out)


def per_device(right_side, blocks, targets, tile_rows, tile_cols):
    col_count = lax.axis_size("col")
    row_count = lax.axis_size("row")
    block_size = blocks.shape[1]
    snapshots = right_side.shape[0]
    row_tiles = right_side.shape[1] // block_size
    own_count = blocks.shape[0]
    capacity = 2 * own_count // col_count
    target = targets[:, 0]
    slot_count = col_count * capacity
    matches = (target[:, None] == jnp.arange(col_count, dtype=jnp.int32)[None, :]).astype(jnp.int32)
    before = jnp.cumsum(matches, axis=0) - matches
    slot_index = target * capacity + jnp.sum(before * matches, axis=1)
    pick = slot_index[:, None] == jnp.arange(slot_count, dtype=jnp.int32)[None, :]
    source = jnp.sum(jnp.where(pick, jnp.arange(own_count, dtype=jnp.int32)[:, None], 0), axis=0)
    source = jnp.where(jnp.any(pick, axis=0), source, own_count)
    padded = jnp.concatenate([blocks, jnp.zeros((1, block_size, block_size), blocks.dtype)], axis=0)
    outgoing = jnp.take(padded, source, axis=0, mode="clip")
    padded_places = jnp.concatenate(
        [jnp.stack([tile_rows, tile_cols], axis=1), jnp.zeros((1, 2), jnp.int32)], axis=0
    )
    places = jnp.take(padded_places, source, axis=0, mode="clip")
    arrived, arrived_places = (
        lax.all_to_all(
            outgoing.reshape(col_count, capacity, block_size, block_size),
            "col",
            split_axis=0,
            concat_axis=0,
            tiled=True,
        ),
        lax.all_to_all(
            places.reshape(col_count, capacity, 2), "col", split_axis=0, concat_axis=0, tiled=True
        ),
    )
    work_blocks = arrived.reshape(col_count * capacity, block_size, block_size)
    flat_places = arrived_places.reshape(col_count * capacity, 2)
    work_rows = flat_places[:, 0]
    work_cols = flat_places[:, 1]

    def backward(left_bf):
        return backward_terms(left_bf, work_blocks, work_rows, work_cols, TC)

    def sum_right(partial_value):
        return big_sum(partial_value, "row")

    def finish_left(unscaled, need_form):
        squares = jnp.sum(unscaled * unscaled, axis=1)
        total = small_sum(squares, "row")
        beta_norm = jnp.sqrt(total + EPSILON)
        scaled = unscaled / beta_norm[:, None]
        rounded = None
        if need_form:
            rounded = scaled.astype(jnp.bfloat16)
        return (beta_norm, scaled, rounded)

    def finish_right(unscaled):
        squares = jnp.sum(unscaled * unscaled, axis=1)
        total = small_sum(squares, "col")
        alpha_norm = jnp.sqrt(total + EPSILON)
        scaled = unscaled / alpha_norm[:, None]
        rounded = scaled.astype(jnp.bfloat16)
        return (alpha_norm, scaled, rounded)

    beta_norm, left_vec, left_bf = finish_left(right_side, True)
    alpha_norm, right_vec, right_bf = finish_right(sum_right(backward(left_bf)))
    search = right_vec
    solution = jnp.zeros_like(right_vec)
    phibar = beta_norm
    rhobar = alpha_norm
    for iteration in range(ITERS):
        last_turn = iteration + 1 == ITERS
        unscaled = (
            big_sum(forward_terms(right_bf, work_blocks, work_rows, work_cols, row_tiles), "col")
            - alpha_norm[:, None] * left_vec
        )
        beta_norm, left_vec, left_bf = finish_left(unscaled, not last_turn)
        rho_value = jnp.sqrt(rhobar * rhobar + beta_norm * beta_norm)
        cosine = rhobar / rho_value
        sine_value = beta_norm / rho_value
        phi_value = cosine * phibar
        phibar = sine_value * phibar
        solution = solution + (phi_value / rho_value)[:, None] * search
        if not last_turn:
            unscaled = sum_right(backward(left_bf)) - beta_norm[:, None] * right_vec
            alpha_norm, right_vec, right_bf = finish_right(unscaled)
            theta_value = sine_value * alpha_norm
            rhobar = -cosine * alpha_norm
            search = right_vec - (theta_value / rho_value)[:, None] * search
    share_len = solution.shape[1] // row_count
    solution = lax.dynamic_slice_in_dim(solution, lax.axis_index("row") * share_len, share_len, 1)
    return (solution.reshape(snapshots, 1, solution.shape[1]), phibar)


def solution(mesh):
    placed = (
        P(None, "row"),
        P(("row", "col"), None, None),
        P(("row", "col"), None),
        P(("row", "col")),
        P(("row", "col")),
    )
    return jax.shard_map(
        per_device,
        mesh=mesh,
        in_specs=placed,
        out_specs=(P(None, "col", "row"), P()),
        check_vma=False,
    )
```

```python
import jax
import jax.numpy as jnp
from jax import lax
from jax.sharding import PartitionSpec as P

TC = 32
ITERS = 4
CHUNKS = 2


EPSILON = 1e-06


def partner_pairs(count, distance):
    return [(i, i ^ distance) for i in range(count)]


def is_power_of_two(count):
    return count & (count - 1) == 0


def small_sum(value, axis):
    count = lax.axis_size(axis)
    if not is_power_of_two(count):
        return lax.psum(value, axis)
    lanes = jnp.split(value, CHUNKS if axis == "col" else 1, axis=0)
    distance = 1
    while distance < count:
        lanes = [lane + lax.ppermute(lane, axis, partner_pairs(count, distance)) for lane in lanes]
        distance *= 2
    return jnp.concatenate(lanes, axis=0)


def big_sum(value, axis):
    count = lax.axis_size(axis)
    width = value.shape[-1]
    if not is_power_of_two(count) or width % (128 * count):
        return lax.psum(value, axis)
    index = lax.axis_index(axis)
    distances = []
    distance = 1
    while distance < count:
        distances.append(distance)
        distance *= 2
    lanes = jnp.split(value, CHUNKS, axis=0)
    last = distances.pop()
    orders = [distances[lane % len(distances):] + distances[:lane % len(distances)] if distances else [] for lane in range(CHUNKS)]
    for step in range(len(distances)):
        moved = []
        for lane, held in enumerate(lanes):
            distance = orders[lane][step]
            upper = (index // distance) % 2
            half = held.shape[-1] // 2
            keep = lax.dynamic_slice_in_dim(held, upper * half, half, held.ndim - 1)
            give = lax.dynamic_slice_in_dim(held, (1 - upper) * half, half, held.ndim - 1)
            moved.append(keep + lax.ppermute(give, axis, partner_pairs(count, distance)))
        lanes = moved
    lanes = [held + lax.ppermute(held, axis, partner_pairs(count, last)) for held in lanes]
    for step in reversed(range(len(distances))):
        moved = []
        for lane, held in enumerate(lanes):
            distance = orders[lane][step]
            upper = (index // distance) % 2
            other = lax.ppermute(held, axis, partner_pairs(count, distance))
            moved.append(jnp.where(
                upper == 1,
                jnp.concatenate([other, held], axis=-1),
                jnp.concatenate([held, other], axis=-1),
            ))
        lanes = moved
    return jnp.concatenate(lanes, axis=0)


def gather_tiles(vector_bf, indices, block_size):
    snapshots, extent = vector_bf.shape
    vector_tiles = vector_bf.reshape(snapshots, extent // block_size, block_size)
    return jnp.take(vector_tiles, indices, axis=1)


def place_terms(weighted, indices, n_out):
    snapshots, number, block_size = weighted.shape
    onehot = (indices[:, None] == jnp.arange(n_out, dtype=jnp.int32)[None, :]).astype(jnp.float32)
    summed = jnp.einsum("ksi,st->kti", weighted, onehot, precision=lax.Precision.HIGH)
    return summed.reshape(snapshots, n_out * block_size)


def forward_terms(vector_bf, blocks, row_index, col_index, n_out):
    picked = gather_tiles(vector_bf, col_index, blocks.shape[1])
    weighted = jnp.einsum("sij,ksj->ksi", blocks, picked, preferred_element_type=jnp.float32)
    return place_terms(weighted, row_index, n_out)


def backward_terms(vector_bf, blocks, row_index, col_index, n_out):
    picked = gather_tiles(vector_bf, row_index, blocks.shape[1])
    weighted = jnp.einsum("sji,ksj->ksi", blocks, picked, preferred_element_type=jnp.float32)
    return place_terms(weighted, col_index, n_out)


def per_device(right_side, blocks, targets, tile_rows, tile_cols):
    col_count = lax.axis_size("col")
    row_count = lax.axis_size("row")
    block_size = blocks.shape[1]
    snapshots = right_side.shape[0]
    row_tiles = right_side.shape[1] // block_size
    own_count = blocks.shape[0]
    capacity = 2 * own_count // col_count
    target = targets[:, 0]
    slot_count = col_count * capacity
    matches = (target[:, None] == jnp.arange(col_count, dtype=jnp.int32)[None, :]).astype(jnp.int32)
    before = jnp.cumsum(matches, axis=0) - matches
    slot_index = target * capacity + jnp.sum(before * matches, axis=1)
    pick = slot_index[:, None] == jnp.arange(slot_count, dtype=jnp.int32)[None, :]
    source = jnp.sum(jnp.where(pick, jnp.arange(own_count, dtype=jnp.int32)[:, None], 0), axis=0)
    source = jnp.where(jnp.any(pick, axis=0), source, own_count)
    padded = jnp.concatenate([blocks, jnp.zeros((1, block_size, block_size), blocks.dtype)], axis=0)
    outgoing = jnp.take(padded, source, axis=0, mode="clip")
    padded_places = jnp.concatenate(
        [jnp.stack([tile_rows, tile_cols], axis=1), jnp.zeros((1, 2), jnp.int32)], axis=0
    )
    places = jnp.take(padded_places, source, axis=0, mode="clip")
    arrived, arrived_places = (
        lax.all_to_all(
            outgoing.reshape(col_count, capacity, block_size, block_size),
            "col",
            split_axis=0,
            concat_axis=0,
            tiled=True,
        ),
        lax.all_to_all(
            places.reshape(col_count, capacity, 2), "col", split_axis=0, concat_axis=0, tiled=True
        ),
    )
    work_blocks = arrived.reshape(col_count * capacity, block_size, block_size)
    flat_places = arrived_places.reshape(col_count * capacity, 2)
    work_rows = flat_places[:, 0]
    work_cols = flat_places[:, 1]

    def backward(left_bf):
        return backward_terms(left_bf, work_blocks, work_rows, work_cols, TC)

    def sum_right(partial_value):
        return big_sum(partial_value, "row")

    def finish_left(unscaled, need_form):
        squares = jnp.sum(unscaled * unscaled, axis=1)
        total = small_sum(squares, "row")
        beta_norm = jnp.sqrt(total + EPSILON)
        scaled = unscaled / beta_norm[:, None]
        rounded = None
        if need_form:
            rounded = scaled.astype(jnp.bfloat16)
        return (beta_norm, scaled, rounded)

    def finish_right(unscaled):
        squares = jnp.sum(unscaled * unscaled, axis=1)
        total = small_sum(squares, "col")
        alpha_norm = jnp.sqrt(total + EPSILON)
        scaled = unscaled / alpha_norm[:, None]
        rounded = scaled.astype(jnp.bfloat16)
        return (alpha_norm, scaled, rounded)

    beta_norm, left_vec, left_bf = finish_left(right_side, True)
    alpha_norm, right_vec, right_bf = finish_right(sum_right(backward(left_bf)))
    search = right_vec
    solution = jnp.zeros_like(right_vec)
    phibar = beta_norm
    rhobar = alpha_norm
    for iteration in range(ITERS):
        last_turn = iteration + 1 == ITERS
        unscaled = (
            big_sum(forward_terms(right_bf, work_blocks, work_rows, work_cols, row_tiles), "col")
            - alpha_norm[:, None] * left_vec
        )
        beta_norm, left_vec, left_bf = finish_left(unscaled, not last_turn)
        rho_value = jnp.sqrt(rhobar * rhobar + beta_norm * beta_norm)
        cosine = rhobar / rho_value
        sine_value = beta_norm / rho_value
        phi_value = cosine * phibar
        phibar = sine_value * phibar
        solution = solution + (phi_value / rho_value)[:, None] * search
        if not last_turn:
            unscaled = sum_right(backward(left_bf)) - beta_norm[:, None] * right_vec
            alpha_norm, right_vec, right_bf = finish_right(unscaled)
            theta_value = sine_value * alpha_norm
            rhobar = -cosine * alpha_norm
            search = right_vec - (theta_value / rho_value)[:, None] * search
    share_len = solution.shape[1] // row_count
    solution = lax.dynamic_slice_in_dim(solution, lax.axis_index("row") * share_len, share_len, 1)
    return (solution.reshape(snapshots, 1, solution.shape[1]), phibar)


def solution(mesh):
    placed = (
        P(None, "row"),
        P(("row", "col"), None, None),
        P(("row", "col"), None),
        P(("row", "col")),
        P(("row", "col")),
    )
    return jax.shard_map(
        per_device,
        mesh=mesh,
        in_specs=placed,
        out_specs=(P(None, "col", "row"), P()),
        check_vma=False,
    )
```
